256 devices in a mesh: req: 32 (over y, x, core), tp: 8 (over z).
Axes of the slice: x: 4, y: 4, z: 8, core: 2. Of those that a mesh axis runs over, the one named last changes fastest.
Arguments:
- tokens: bfloat16 [256, 4, 1536], P('req'), may hold values from -6 to 6
- lengths: int32 [256], P('req'), may hold values from 16 to 32768, as said below
- page_table: int32 [256, 9], P('req'), may hold values from 0 to 2303, as said below
- kv_pages: bfloat16 [2304, 2, 128, 128], P('req'), may hold values from -480 to 480
- norm_gain: float32 [1536], replicated, may hold values from 0.1 to 1.9
- query_weight: bfloat16 [1536, 1024], P(None, 'tp'), may hold values from -0.15625 to 0.15625
- key_weight: bfloat16 [1536, 128], replicated, may hold values from -0.15625 to 0.15625
- value_weight: bfloat16 [1536, 128], replicated, may hold values from -0.15625 to 0.15625
- out_weight: bfloat16 [1024, 1536], P('tp'), may hold values from -0.1875 to 0.1875
- mlp_gain: float32 [1536], replicated, may hold values from 0.1 to 1.9
- gate_weight: bfloat16 [1536, 4608], P(None, 'tp'), may hold values from -0.15625 to 0.15625
- up_weight: bfloat16 [1536, 4608], P(None, 'tp'), may hold values from -0.15625 to 0.15625
- down_weight: bfloat16 [4608, 1536], P('tp'), may hold values from -0.09375 to 0.09375
Outputs:
- layer_out: bfloat16 [256, 4, 1536], P('req')
The draws below stay inside these ranges and needn't reach their ends.
Inputs may be any that keep to these rules, and one draw needn't show every extreme that they name: `lengths`: one request has exactly 32768 cached positions in every draw. `page_table`: all entries together are a permutation of the 2304 pool pages. Entry (r, j) is pool page r * 9 + j, in the part of the pool held with request r, except for spilled entries chosen from the seed (about a fifth of all); the spilled entries hold one another's pool pages in an order drawn from the seed, mostly on other devices of req.
All inputs are finite; a program needn't handle non-finite values.
Results may differ from the reference program's by a relative error of at most 0.0095.
The reference program's roundings to bfloat16 on the way count: a program that leaves them out, or rounds other values in their place, can miss the bound.
Values may be sent and summed in bfloat16 or wider, within the bound.
No kernel may reach another device: no remote copies, remote signals or barrier semaphores. Data moves between devices by JAX's collectives and lax.ppermute only.
A program may use at most 128 MiB of HBM per device.

```python
import math
import jax
import jax.numpy as jnp
from jax import lax

D = 1536
HEADS = 8
HD = 128
FF = 4608
WINDOW = 1024
PAGE = 128
STEPS = 4
MAX_LEN = 32768
REQUESTS = 256
WP = 9
NPAGE = 2304


def draw_lengths(key, part):
    key_exp, key_off, key_top = jax.random.split(jax.random.fold_in(key, 11), 3)
    exponent = jax.random.randint(key_exp, (REQUESTS,), 4, 15)
    base_len = jnp.left_shift(jnp.ones((REQUESTS,), jnp.int32), exponent)
    offset = jax.random.randint(key_off, (REQUESTS,), 0, base_len)
    longest = jax.random.randint(key_top, (), 0, REQUESTS)
    return (base_len + offset).at[longest].set(MAX_LEN).astype(jnp.int32)


def draw_page_table(key, part):
    key_pick, key_order = jax.random.split(jax.random.fold_in(key, 23), 2)
    index = jnp.arange(NPAGE, dtype=jnp.int32)
    spilled = jax.random.randint(key_pick, (NPAGE,), 0, 5) == 0
    stay = jnp.where(spilled, 0, 1).astype(jnp.int32)
    shuffled = jax.random.permutation(key_order, NPAGE).astype(jnp.int32)
    slot_order = jnp.argsort(stay * NPAGE + index, stable=True).astype(jnp.int32)
    value_order = jnp.argsort(stay * NPAGE + jnp.where(spilled, shuffled, index), stable=True).astype(jnp.int32)
    table = jnp.zeros((NPAGE,), jnp.int32).at[slot_order].set(value_order)
    return table.reshape(REQUESTS, WP)


def draw_kv_pages(key, part):
    key_k, key_v, key_s = jax.random.split(jax.random.fold_in(key, 37), 3)
    keys = jax.random.truncated_normal(key_k, -4.0, 4.0, (NPAGE, 1, PAGE, HD), jnp.float32)
    values = jax.random.truncated_normal(key_v, -4.0, 4.0, (NPAGE, 1, PAGE, HD), jnp.float32)
    scale = jnp.exp(jax.random.uniform(key_s, (NPAGE, 1, 1, 1), jnp.float32, math.log(0.5), math.log(2.0)))
    return jnp.concatenate([keys * scale, values], axis=1).astype(jnp.bfloat16)


def block_levels(own_key, shape, pieces, low, high):
    def one(dim, blocks):
        draws = jax.random.uniform(jax.random.fold_in(jax.random.fold_in(own_key, 6), dim), (blocks,), jnp.float32, low / len(pieces), high / len(pieces))
        return jnp.repeat(jnp.exp(draws), shape[dim] // blocks).reshape((-1,) + (1,) * (len(shape) - dim - 1))

    level = one(*pieces[0])
    for cut in pieces[1:]:
        level = level * one(*cut)
    return level


def centred(own_key, dims, spread, bound, cuts=(), held_as=jnp.bfloat16):
    level = block_levels(own_key, dims, cuts, -0.22, 0.18) if cuts else 1.0
    result = jax.random.normal(own_key, dims, jnp.float32) * spread * level
    return jnp.minimum(jnp.maximum(result, -bound), bound).astype(held_as)


def setup_inputs(seed: int = 0) -> dict:
    seeds = jax.random.split(jax.random.key(seed), 14)
    tokens = centred(seeds[0], (REQUESTS, STEPS, D), 1.0, 6.0, ((0, 32),))
    lengths = draw_lengths(jax.random.fold_in(seeds[13], 71), 0)
    page_table = draw_page_table(jax.random.fold_in(seeds[13], 71), 0)
    kv_pages = draw_kv_pages(jax.random.fold_in(seeds[13], 71), 0)
    norm_gain = jnp.clip(1.0 + 0.18 * jax.random.normal(seeds[4], (D,), jnp.float32), 0.1, 1.9)
    query_weight = centred(seeds[5], (D, HEADS * HD), D ** -0.5, 0.15625, ((1, 8),))
    key_weight = centred(seeds[6], (D, HD), D ** -0.5, 0.15625)
    value_weight = centred(seeds[7], (D, HD), D ** -0.5, 0.15625)
    out_weight = centred(seeds[8], (HEADS * HD, D), (HEADS * HD) ** -0.5, 0.1875, ((0, 8),))
    mlp_gain = jnp.clip(1.0 + 0.18 * jax.random.normal(seeds[9], (D,), jnp.float32), 0.1, 1.9)
    gate_weight = centred(seeds[10], (D, FF), D ** -0.5, 0.15625, ((1, 8),))
    up_weight = centred(seeds[11], (D, FF), D ** -0.5, 0.15625, ((1, 8),))
    down_weight = centred(seeds[12], (FF, D), FF ** -0.5, 0.09375, ((0, 8),))
    return {"tokens": tokens, "lengths": lengths, "page_table": page_table, "kv_pages": kv_pages, "norm_gain": norm_gain, "query_weight": query_weight, "key_weight": key_weight, "value_weight": value_weight, "out_weight": out_weight, "mlp_gain": mlp_gain, "gate_weight": gate_weight, "up_weight": up_weight, "down_weight": down_weight}


negative = -1e+30
epsilon = 1e-06

def rms_norm(values, gain):
    return values * lax.rsqrt(lax.optimization_barrier(jnp.mean(values * values, axis=-1, keepdims=True)) + epsilon) * gain

def reference(tokens, lengths, page_table, kv_pages, norm_gain, query_weight, key_weight, value_weight, out_weight, mlp_gain, gate_weight, up_weight, down_weight):
    token_rows = tokens.reshape(REQUESTS * STEPS, D)
    normed = rms_norm(token_rows.astype(jnp.float32), norm_gain).astype(jnp.bfloat16)
    queries = (jnp.dot(normed, query_weight, preferred_element_type=jnp.float32) * HD ** (-0.5)).astype(jnp.bfloat16)
    key_new = jnp.dot(normed, key_weight, preferred_element_type=jnp.float32).astype(jnp.bfloat16)
    value_new = jnp.dot(normed, value_weight, preferred_element_type=jnp.float32).astype(jnp.bfloat16)
    queries = queries.reshape(REQUESTS, STEPS, HEADS, HD)
    key_new = key_new.reshape(REQUESTS, STEPS, HD)
    value_new = value_new.reshape(REQUESTS, STEPS, HD)

    def attend_one(request_item):
        query_one, key_one, value_one, length, table = request_item
        pages = kv_pages[table].astype(jnp.float32)
        first_page = jnp.maximum(length - (WINDOW - 1), 0) // PAGE
        position = (first_page + jnp.arange(WP, dtype=jnp.int32))[:, None] * PAGE + jnp.arange(PAGE, dtype=jnp.int32)[None, :]
        current = length + jnp.arange(STEPS, dtype=jnp.int32)
        visible = (position[None] < length) & (position[None] > current[:, None, None] - WINDOW)
        visible = visible[:, :, None, :]
        scores = jnp.einsum('shd,wpd->swhp', query_one.astype(jnp.float32), pages[:, 0])
        scores = jnp.where(visible, scores, negative)
        block_max = lax.optimization_barrier(jnp.max(scores, axis=-1))
        weights = jnp.where(visible, jnp.exp(scores - block_max[..., None]), 0.0)
        block_total = lax.optimization_barrier(jnp.sum(weights, axis=-1))
        rounded = lax.optimization_barrier(weights.astype(jnp.bfloat16)).astype(jnp.float32)
        block_out = jnp.einsum('swhp,wpd->swhd', rounded, pages[:, 1])
        new_scores = jnp.einsum('shd,td->sht', query_one.astype(jnp.float32), key_one.astype(jnp.float32))
        causal = (jnp.arange(STEPS)[None, :] <= jnp.arange(STEPS)[:, None])[:, None, :]
        new_scores = jnp.where(causal, new_scores, negative)
        new_max = lax.optimization_barrier(jnp.max(new_scores, axis=-1))
        new_weights = jnp.where(causal, jnp.exp(new_scores - new_max[..., None]), 0.0)
        new_total = lax.optimization_barrier(jnp.sum(new_weights, axis=-1))
        new_rounded = lax.optimization_barrier(new_weights.astype(jnp.bfloat16)).astype(jnp.float32)
        new_out = jnp.einsum('sht,td->shd', new_rounded, value_one.astype(jnp.float32))
        overall = jnp.maximum(lax.optimization_barrier(jnp.max(block_max, axis=1)), new_max)
        cache_scale = jnp.exp(block_max - overall[:, None])
        new_scale = jnp.exp(new_max - overall)
        total = lax.optimization_barrier(jnp.sum(block_total * cache_scale, axis=1)) + new_total * new_scale
        summed = lax.optimization_barrier(jnp.sum(block_out * cache_scale[..., None], axis=1)) + new_out * new_scale[..., None]
        return (summed / total[..., None]).astype(jnp.bfloat16).reshape(STEPS, HEADS * HD)
    attended = lax.map(attend_one, (queries, key_new, value_new, lengths, page_table))
    attended = attended.reshape(REQUESTS * STEPS, HEADS * HD)
    projected = jnp.dot(attended, out_weight, preferred_element_type=jnp.float32)
    residual = (token_rows.astype(jnp.float32) + projected).astype(jnp.bfloat16)
    mlp_in = rms_norm(residual.astype(jnp.float32), mlp_gain).astype(jnp.bfloat16)
    gate = jnp.dot(mlp_in, gate_weight, preferred_element_type=jnp.float32)
    upward = jnp.dot(mlp_in, up_weight, preferred_element_type=jnp.float32)
    hidden = (jax.nn.gelu(gate, approximate=True) * upward).astype(jnp.bfloat16)
    mlp_out = jnp.dot(hidden, down_weight, preferred_element_type=jnp.float32)
    layer_out = (residual.astype(jnp.float32) + mlp_out).astype(jnp.bfloat16)
    return layer_out.reshape(REQUESTS, STEPS, D)
```

```python
import jax
import jax.numpy as jnp
from jax import lax
from jax.sharding import PartitionSpec as P

WINDOW = 1024


negative = -1e30
epsilon = 1e-06


def rms_norm(values, gain):
    return values * lax.rsqrt(jnp.mean(values * values, axis=-1, keepdims=True) + epsilon) * gain


def tree_sum(values, axis, size):
    step = 1
    while step < size:
        values = values + lax.ppermute(values, axis, [(i, i ^ step) for i in range(size)])
        step *= 2
    return values


def make_body(req_size, tp_size):
    def body(
        tokens,
        lengths,
        page_table,
        kv_pages,
        norm_gain,
        query_weight,
        key_weight,
        value_weight,
        out_weight,
        mlp_gain,
        gate_weight,
        up_weight,
        down_weight,
    ):
        req_dev, steps, width = tokens.shape
        head_dim = key_weight.shape[1]
        heads_dev = query_weight.shape[1] // head_dim
        pool_size = kv_pages.shape[0]
        page_size = kv_pages.shape[2]
        window_pages = page_table.shape[1]
        requests = req_dev * req_size
        qwidth = steps * heads_dev * head_dim
        token_rows = tokens.reshape(req_dev * steps, width)
        normed = rms_norm(token_rows.astype(jnp.float32), norm_gain).astype(jnp.bfloat16)
        queries = (
            jnp.dot(normed, query_weight, preferred_element_type=jnp.float32) * head_dim ** (-0.5)
        ).astype(jnp.bfloat16)
        key_new = jnp.dot(normed, key_weight, preferred_element_type=jnp.float32).astype(jnp.bfloat16)
        value_new = jnp.dot(normed, value_weight, preferred_element_type=jnp.float32).astype(
            jnp.bfloat16
        )
        packed = jnp.concatenate(
            [
                queries.reshape(req_dev, qwidth).astype(jnp.float32),
                page_table.astype(jnp.float32),
                lengths.reshape(req_dev, 1).astype(jnp.float32),
            ],
            axis=1,
        )
        gathered = lax.all_gather(packed, "req", axis=0, tiled=True)
        all_queries = gathered[:, :qwidth].astype(jnp.bfloat16).reshape(
            requests, steps * heads_dev, head_dim
        )
        all_table = gathered[:, qwidth : qwidth + window_pages].astype(jnp.int32)
        all_lengths = gathered[:, qwidth + window_pages].astype(jnp.int32)
        flat_table = all_table.reshape(-1)
        entries = flat_table.shape[0]
        my_slots = lax.axis_index("req") * pool_size + jnp.arange(pool_size, dtype=jnp.int32)
        match = flat_table[None, :] == my_slots[:, None]
        owner_entry = jnp.sum(
            jnp.where(match, jnp.arange(entries, dtype=jnp.int32)[None, :], 0), axis=1
        )
        page_request = owner_entry // window_pages
        page_number = owner_entry % window_pages
        page_length = all_lengths[page_request]
        first_page = jnp.maximum(page_length - (WINDOW - 1), 0) // page_size
        position = (first_page + page_number)[:, None] * page_size + jnp.arange(
            page_size, dtype=jnp.int32
        )[None, :]
        current = page_length[:, None] + jnp.arange(steps, dtype=jnp.int32)[None, :]
        visible = (position[:, None, :] < page_length[:, None, None]) & (
            position[:, None, :] > current[:, :, None] - WINDOW
        )
        visible = visible[:, :, None, :]
        page_queries = all_queries[page_request]
        scores = jnp.einsum(
            "pqd,pkd->pqk", page_queries, kv_pages[:, 0], preferred_element_type=jnp.float32
        )
        scores = jnp.where(visible, scores.reshape(pool_size, steps, heads_dev, page_size), negative)
        block_max = jnp.max(scores, axis=-1)
        weights = jnp.where(visible, jnp.exp(scores - block_max[..., None]), 0.0)
        block_total = jnp.sum(weights, axis=-1)
        block_out = jnp.einsum(
            "pqk,pkd->pqd",
            weights.astype(jnp.bfloat16).reshape(pool_size, steps * heads_dev, page_size),
            kv_pages[:, 1],
            preferred_element_type=jnp.float32,
        )
        block_out = block_out.reshape(pool_size, steps, heads_dev, head_dim)
        member = page_request[None, :] == jnp.arange(requests, dtype=jnp.int32)[:, None]
        local_max = jnp.max(
            jnp.where(member[:, :, None, None], block_max[None], negative), axis=1
        )
        scale = jnp.exp(block_max - local_max[page_request])
        sent_out = jax.ops.segment_sum(
            block_out * scale[..., None], page_request, num_segments=requests
        )
        sent_total = jax.ops.segment_sum(block_total * scale, page_request, num_segments=requests)
        nsh = steps * heads_dev
        send = jnp.concatenate(
            [
                sent_out.reshape(requests, nsh * head_dim),
                sent_total.reshape(requests, nsh),
                local_max.reshape(requests, nsh),
            ],
            axis=1,
        )
        recv = lax.all_to_all(send, "req", 0, 0, tiled=True).reshape(req_size, req_dev, -1)
        got_out = recv[:, :, : nsh * head_dim].reshape(req_size, req_dev, steps, heads_dev, head_dim)
        got_total = recv[:, :, nsh * head_dim : nsh * (head_dim + 1)].reshape(
            req_size, req_dev, steps, heads_dev
        )
        got_max = recv[:, :, nsh * (head_dim + 1) :].reshape(req_size, req_dev, steps, heads_dev)
        cache_max = jnp.max(got_max, axis=0)
        local_queries = queries.reshape(req_dev, steps, heads_dev, head_dim)
        new_scores = jnp.einsum(
            "rshd,rtd->rsht",
            local_queries,
            key_new.reshape(req_dev, steps, head_dim),
            preferred_element_type=jnp.float32,
        )
        causal = (jnp.arange(steps)[None, :] <= jnp.arange(steps)[:, None])[None, :, None, :]
        new_scores = jnp.where(causal, new_scores, negative)
        new_max = jnp.max(new_scores, axis=-1)
        new_weights = jnp.where(causal, jnp.exp(new_scores - new_max[..., None]), 0.0)
        new_total = jnp.sum(new_weights, axis=-1)
        new_out = jnp.einsum(
            "rsht,rtd->rshd",
            new_weights.astype(jnp.bfloat16),
            value_new.reshape(req_dev, steps, head_dim),
            preferred_element_type=jnp.float32,
        )
        overall = jnp.maximum(cache_max, new_max)
        src_scale = jnp.exp(got_max - overall[None])
        new_scale = jnp.exp(new_max - overall)
        total = jnp.sum(got_total * src_scale, axis=0) + new_total * new_scale
        summed = jnp.sum(got_out * src_scale[..., None], axis=0) + new_out * new_scale[..., None]
        attended = (
            (summed / total[..., None])
            .astype(jnp.bfloat16)
            .reshape(req_dev * steps, heads_dev * head_dim)
        )
        projected = jnp.dot(attended, out_weight, preferred_element_type=jnp.float32)
        attn_total = tree_sum(projected, "tp", tp_size)
        residual = (token_rows.astype(jnp.float32) + attn_total).astype(jnp.bfloat16)
        mlp_in = rms_norm(residual.astype(jnp.float32), mlp_gain).astype(jnp.bfloat16)
        gate = jnp.dot(mlp_in, gate_weight, preferred_element_type=jnp.float32)
        upward = jnp.dot(mlp_in, up_weight, preferred_element_type=jnp.float32)
        hidden = (jax.nn.gelu(gate, approximate=True) * upward).astype(jnp.bfloat16)
        mlp_part = jnp.dot(hidden, down_weight, preferred_element_type=jnp.float32).astype(
            jnp.bfloat16
        )
        mlp_total = tree_sum(mlp_part, "tp", tp_size).astype(jnp.float32)
        layer_out = (residual.astype(jnp.float32) + mlp_total).astype(jnp.bfloat16)
        return layer_out.reshape(req_dev, steps, width)

    return body


def solution(mesh):
    return jax.shard_map(
        make_body(mesh.shape["req"], mesh.shape["tp"]),
        mesh=mesh,
        in_specs=(
            P("req", None, None),
            P("req"),
            P("req", None),
            P("req", None, None, None),
            P(),
            P(None, "tp"),
            P(),
            P(),
            P("tp", None),
            P(),
            P(None, "tp"),
            P(None, "tp"),
            P("tp", None),
        ),
        out_specs=P("req", None, None),
        check_vma=False,
    )
```

```python
import jax
import jax.numpy as jnp
from jax import lax
from jax.sharding import PartitionSpec as P

WINDOW = 1024


negative = -1e30
epsilon = 1e-06


def rms_norm(values, gain):
    return values * lax.rsqrt(jnp.mean(values * values, axis=-1, keepdims=True) + epsilon) * gain


def tree_sum(values, axis, size):
    step = 1
    while step < size:
        values = values + lax.ppermute(values, axis, [(i, i ^ step) for i in range(size)])
        step *= 2
    return values


def tree_gather(values, axis, size):
    index = lax.axis_index(axis)
    parts = values[None]
    step = 1
    while step < size:
        other = lax.ppermute(parts, axis, [(i, i ^ step) for i in range(size)])
        upper = (index // step) % 2 == 1
        parts = jnp.concatenate(
            [jnp.where(upper, other, parts), jnp.where(upper, parts, other)], axis=0
        )
        step *= 2
    return parts


def make_body(req_size, tp_size):
    def body(
        tokens,
        lengths,
        page_table,
        kv_pages,
        norm_gain,
        query_weight,
        key_weight,
        value_weight,
        out_weight,
        mlp_gain,
        gate_weight,
        up_weight,
        down_weight,
    ):
        req_dev, steps, width = tokens.shape
        head_dim = key_weight.shape[1]
        heads_dev = query_weight.shape[1] // head_dim
        pool_size = kv_pages.shape[0]
        page_size = kv_pages.shape[2]
        window_pages = page_table.shape[1]
        requests = req_dev * req_size
        qwidth = steps * heads_dev * head_dim
        token_rows = tokens.reshape(req_dev * steps, width)
        full_out_weight = lax.all_gather(out_weight, "tp", axis=0, tiled=True)
        normed = rms_norm(token_rows.astype(jnp.float32), norm_gain).astype(jnp.bfloat16)
        queries = (
            jnp.dot(normed, query_weight, preferred_element_type=jnp.float32) * head_dim ** (-0.5)
        ).astype(jnp.bfloat16)
        key_new = jnp.dot(normed, key_weight, preferred_element_type=jnp.float32).astype(jnp.bfloat16)
        value_new = jnp.dot(normed, value_weight, preferred_element_type=jnp.float32).astype(
            jnp.bfloat16
        )
        packed = jnp.concatenate(
            [
                queries.reshape(req_dev, qwidth).astype(jnp.float32),
                page_table.astype(jnp.float32),
                lengths.reshape(req_dev, 1).astype(jnp.float32),
            ],
            axis=1,
        )
        gathered = lax.all_to_all(
            jnp.broadcast_to(packed[None], (req_size,) + packed.shape), "req", 0, 0, tiled=False
        ).reshape(requests, packed.shape[1])
        all_queries = gathered[:, :qwidth].astype(jnp.bfloat16).reshape(
            requests, steps * heads_dev, head_dim
        )
        all_table = gathered[:, qwidth : qwidth + window_pages].astype(jnp.int32)
        all_lengths = gathered[:, qwidth + window_pages].astype(jnp.int32)
        flat_table = all_table.reshape(-1)
        entries = flat_table.shape[0]
        my_slots = lax.axis_index("req") * pool_size + jnp.arange(pool_size, dtype=jnp.int32)
        match = flat_table[None, :] == my_slots[:, None]
        owner_entry = jnp.sum(
            jnp.where(match, jnp.arange(entries, dtype=jnp.int32)[None, :], 0), axis=1
        )
        page_request = owner_entry // window_pages
        page_number = owner_entry % window_pages
        page_length = all_lengths[page_request]
        first_page = jnp.maximum(page_length - (WINDOW - 1), 0) // page_size
        position = (first_page + page_number)[:, None] * page_size + jnp.arange(
            page_size, dtype=jnp.int32
        )[None, :]
        current = page_length[:, None] + jnp.arange(steps, dtype=jnp.int32)[None, :]
        visible = (position[:, None, :] < page_length[:, None, None]) & (
            position[:, None, :] > current[:, :, None] - WINDOW
        )
        visible = visible[:, :, None, :]
        page_queries = all_queries[page_request]
        scores = jnp.einsum(
            "pqd,pkd->pqk", page_queries, kv_pages[:, 0], preferred_element_type=jnp.float32
        )
        scores = jnp.where(visible, scores.reshape(pool_size, steps, heads_dev, page_size), negative)
        block_max = jnp.max(scores, axis=-1)
        weights = jnp.where(visible, jnp.exp(scores - block_max[..., None]), 0.0)
        block_total = jnp.sum(weights, axis=-1)
        block_out = jnp.einsum(
            "pqk,pkd->pqd",
            weights.astype(jnp.bfloat16).reshape(pool_size, steps * heads_dev, page_size),
            kv_pages[:, 1],
            preferred_element_type=jnp.float32,
        )
        block_out = block_out.reshape(pool_size, steps, heads_dev, head_dim)
        member = page_request[None, :] == jnp.arange(requests, dtype=jnp.int32)[:, None]
        local_max = jnp.max(
            jnp.where(member[:, :, None, None], block_max[None], negative), axis=1
        )
        scale = jnp.exp(block_max - local_max[page_request])
        sent_out = jax.ops.segment_sum(
            block_out * scale[..., None], page_request, num_segments=requests
        )
        sent_total = jax.ops.segment_sum(block_total * scale, page_request, num_segments=requests)
        nsh = steps * heads_dev
        send = jnp.concatenate(
            [
                sent_out.reshape(requests, nsh * head_dim),
                sent_total.reshape(requests, nsh),
                local_max.reshape(requests, nsh),
            ],
            axis=1,
        )
        recv = lax.all_to_all(send, "req", 0, 0, tiled=True).reshape(req_size, req_dev, -1)
        got_out = recv[:, :, : nsh * head_dim].reshape(req_size, req_dev, steps, heads_dev, head_dim)
        got_total = recv[:, :, nsh * head_dim : nsh * (head_dim + 1)].reshape(
            req_size, req_dev, steps, heads_dev
        )
        got_max = recv[:, :, nsh * (head_dim + 1) :].reshape(req_size, req_dev, steps, heads_dev)
        cache_max = jnp.max(got_max, axis=0)
        local_queries = queries.reshape(req_dev, steps, heads_dev, head_dim)
        new_scores = jnp.einsum(
            "rshd,rtd->rsht",
            local_queries,
            key_new.reshape(req_dev, steps, head_dim),
            preferred_element_type=jnp.float32,
        )
        causal = (jnp.arange(steps)[None, :] <= jnp.arange(steps)[:, None])[None, :, None, :]
        new_scores = jnp.where(causal, new_scores, negative)
        new_max = jnp.max(new_scores, axis=-1)
        new_weights = jnp.where(causal, jnp.exp(new_scores - new_max[..., None]), 0.0)
        new_total = jnp.sum(new_weights, axis=-1)
        new_out = jnp.einsum(
            "rsht,rtd->rshd",
            new_weights.astype(jnp.bfloat16),
            value_new.reshape(req_dev, steps, head_dim),
            preferred_element_type=jnp.float32,
        )
        overall = jnp.maximum(cache_max, new_max)
        src_scale = jnp.exp(got_max - overall[None])
        new_scale = jnp.exp(new_max - overall)
        total = jnp.sum(got_total * src_scale, axis=0) + new_total * new_scale
        summed = jnp.sum(got_out * src_scale[..., None], axis=0) + new_out * new_scale[..., None]
        attended = (
            (summed / total[..., None])
            .astype(jnp.bfloat16)
            .reshape(req_dev * steps, heads_dev * head_dim)
        )
        all_heads = tree_gather(attended, "tp", tp_size)
        all_heads = jnp.moveaxis(all_heads, 0, 1).reshape(req_dev * steps, -1)
        attn_total = jnp.dot(all_heads, full_out_weight, preferred_element_type=jnp.float32)
        residual = (token_rows.astype(jnp.float32) + attn_total).astype(jnp.bfloat16)
        mlp_in = rms_norm(residual.astype(jnp.float32), mlp_gain).astype(jnp.bfloat16)
        gate = jnp.dot(mlp_in, gate_weight, preferred_element_type=jnp.float32)
        upward = jnp.dot(mlp_in, up_weight, preferred_element_type=jnp.float32)
        hidden = (jax.nn.gelu(gate, approximate=True) * upward).astype(jnp.bfloat16)
        mlp_part = jnp.dot(hidden, down_weight, preferred_element_type=jnp.float32).astype(
            jnp.bfloat16
        )
        mlp_total = tree_sum(mlp_part, "tp", tp_size).astype(jnp.float32)
        layer_out = (residual.astype(jnp.float32) + mlp_total).astype(jnp.bfloat16)
        return layer_out.reshape(req_dev, steps, width)

    return body


def solution(mesh):
    return jax.shard_map(
        make_body(mesh.shape["req"], mesh.shape["tp"]),
        mesh=mesh,
        in_specs=(
            P("req", None, None),
            P("req"),
            P("req", None),
            P("req", None, None, None),
            P(),
            P(None, "tp"),
            P(),
            P(),
            P("tp", None),
            P(),
            P(None, "tp"),
            P(None, "tp"),
            P("tp", None),
        ),
        out_specs=P("req", None, None),
        check_vma=False,
    )
```

```python
import jax
import jax.numpy as jnp
from jax import lax
from jax.sharding import PartitionSpec as P

WINDOW = 1024


negative = -1e30
epsilon = 1e-06


def rms_norm(values, gain):
    return values * lax.rsqrt(jnp.mean(values * values, axis=-1, keepdims=True) + epsilon) * gain


def tree_sum(values, axis, size):
    step = 1
    while step < size:
        values = values + lax.ppermute(values, axis, [(i, i ^ step) for i in range(size)])
        step *= 2
    return values


def tree_gather(values, axis, size):
    index = lax.axis_index(axis)
    parts = values[None]
    step = 1
    while step < size:
        other = lax.ppermute(parts, axis, [(i, i ^ step) for i in range(size)])
        upper = (index // step) % 2 == 1
        parts = jnp.concatenate(
            [jnp.where(upper, other, parts), jnp.where(upper, parts, other)], axis=0
        )
        step *= 2
    return parts


def make_body(req_size, tp_size):
    def body(
        tokens,
        lengths,
        page_table,
        kv_pages,
        norm_gain,
        query_weight,
        key_weight,
        value_weight,
        out_weight,
        mlp_gain,
        gate_weight,
        up_weight,
        down_weight,
    ):
        req_dev, steps, width = tokens.shape
        head_dim = key_weight.shape[1]
        heads_dev = query_weight.shape[1] // head_dim
        pool_size = kv_pages.shape[0]
        page_size = kv_pages.shape[2]
        window_pages = page_table.shape[1]
        requests = req_dev * req_size
        qwidth = steps * heads_dev * head_dim
        token_rows = tokens.reshape(req_dev * steps, width)
        full_out_weight = lax.all_gather(out_weight, "tp", axis=0, tiled=True)
        normed = rms_norm(token_rows.astype(jnp.float32), norm_gain).astype(jnp.bfloat16)
        queries = (
            jnp.dot(normed, query_weight, preferred_element_type=jnp.float32) * head_dim ** (-0.5)
        ).astype(jnp.bfloat16)
        key_new = jnp.dot(normed, key_weight, preferred_element_type=jnp.float32).astype(jnp.bfloat16)
        value_new = jnp.dot(normed, value_weight, preferred_element_type=jnp.float32).astype(
            jnp.bfloat16
        )
        ints = jnp.concatenate([page_table, lengths.reshape(req_dev, 1)], axis=1)
        packed = jnp.concatenate(
            [
                queries.reshape(req_dev, qwidth),
                (ints // 256).astype(jnp.bfloat16),
                (ints % 256).astype(jnp.bfloat16),
            ],
            axis=1,
        )
        gathered = lax.all_to_all(
            jnp.broadcast_to(packed[None], (req_size,) + packed.shape), "req", 0, 0, tiled=False
        ).reshape(requests, packed.shape[1])
        all_queries = gathered[:, :qwidth].reshape(requests, steps * heads_dev, head_dim)
        nints = window_pages + 1
        digits = gathered[:, qwidth:].astype(jnp.int32)
        all_ints = digits[:, :nints] * 256 + digits[:, nints:]
        all_table = all_ints[:, :window_pages]
        all_lengths = all_ints[:, window_pages]
        flat_table = all_table.reshape(-1)
        entries = flat_table.shape[0]
        my_slots = lax.axis_index("req") * pool_size + jnp.arange(pool_size, dtype=jnp.int32)
        match = flat_table[None, :] == my_slots[:, None]
        owner_entry = jnp.sum(
            jnp.where(match, jnp.arange(entries, dtype=jnp.int32)[None, :], 0), axis=1
        )
        page_request = owner_entry // window_pages
        page_number = owner_entry % window_pages
        page_length = all_lengths[page_request]
        first_page = jnp.maximum(page_length - (WINDOW - 1), 0) // page_size
        position = (first_page + page_number)[:, None] * page_size + jnp.arange(
            page_size, dtype=jnp.int32
        )[None, :]
        current = page_length[:, None] + jnp.arange(steps, dtype=jnp.int32)[None, :]
        visible = (position[:, None, :] < page_length[:, None, None]) & (
            position[:, None, :] > current[:, :, None] - WINDOW
        )
        visible = visible[:, :, None, :]
        page_queries = all_queries[page_request]
        scores = jnp.einsum(
            "pqd,pkd->pqk", page_queries, kv_pages[:, 0], preferred_element_type=jnp.float32
        )
        scores = jnp.where(visible, scores.reshape(pool_size, steps, heads_dev, page_size), negative)
        block_max = jnp.max(scores, axis=-1)
        weights = jnp.where(visible, jnp.exp(scores - block_max[..., None]), 0.0)
        block_total = jnp.sum(weights, axis=-1)
        block_out = jnp.einsum(
            "pqk,pkd->pqd",
            weights.astype(jnp.bfloat16).reshape(pool_size, steps * heads_dev, page_size),
            kv_pages[:, 1],
            preferred_element_type=jnp.float32,
        )
        block_out = block_out.reshape(pool_size, steps, heads_dev, head_dim)
        member = page_request[None, :] == jnp.arange(requests, dtype=jnp.int32)[:, None]
        local_max = jnp.max(
            jnp.where(member[:, :, None, None], block_max[None], negative), axis=1
        )
        scale = jnp.exp(block_max - local_max[page_request])
        nsh = steps * heads_dev
        scaled = jnp.concatenate(
            [
                (block_out * scale[..., None]).reshape(pool_size, nsh * head_dim),
                (block_total * scale).reshape(pool_size, nsh),
            ],
            axis=1,
        )
        sent = jnp.dot(
            member.astype(jnp.float32),
            scaled,
            precision=lax.Precision.HIGHEST,
            preferred_element_type=jnp.float32,
        )
        send = jnp.concatenate([sent, local_max.reshape(requests, nsh)], axis=1)
        recv = lax.all_to_all(send, "req", 0, 0, tiled=True).reshape(req_size, req_dev, -1)
        got_out = recv[:, :, : nsh * head_dim].reshape(req_size, req_dev, steps, heads_dev, head_dim)
        got_total = recv[:, :, nsh * head_dim : nsh * (head_dim + 1)].reshape(
            req_size, req_dev, steps, heads_dev
        )
        got_max = recv[:, :, nsh * (head_dim + 1) :].reshape(req_size, req_dev, steps, heads_dev)
        cache_max = jnp.max(got_max, axis=0)
        local_queries = queries.reshape(req_dev, steps, heads_dev, head_dim)
        new_scores = jnp.einsum(
            "rshd,rtd->rsht",
            local_queries,
            key_new.reshape(req_dev, steps, head_dim),
            preferred_element_type=jnp.float32,
        )
        causal = (jnp.arange(steps)[None, :] <= jnp.arange(steps)[:, None])[None, :, None, :]
        new_scores = jnp.where(causal, new_scores, negative)
        new_max = jnp.max(new_scores, axis=-1)
        new_weights = jnp.where(causal, jnp.exp(new_scores - new_max[..., None]), 0.0)
        new_total = jnp.sum(new_weights, axis=-1)
        new_out = jnp.einsum(
            "rsht,rtd->rshd",
            new_weights.astype(jnp.bfloat16),
            value_new.reshape(req_dev, steps, head_dim),
            preferred_element_type=jnp.float32,
        )
        overall = jnp.maximum(cache_max, new_max)
        src_scale = jnp.exp(got_max - overall[None])
        new_scale = jnp.exp(new_max - overall)
        total = jnp.sum(got_total * src_scale, axis=0) + new_total * new_scale
        summed = jnp.sum(got_out * src_scale[..., None], axis=0) + new_out * new_scale[..., None]
        attended = (
            (summed / total[..., None])
            .astype(jnp.bfloat16)
            .reshape(req_dev * steps, heads_dev * head_dim)
        )
        all_heads = tree_gather(attended, "tp", tp_size)
        all_heads = jnp.moveaxis(all_heads, 0, 1).reshape(req_dev * steps, -1)
        attn_total = jnp.dot(all_heads, full_out_weight, preferred_element_type=jnp.float32)
        residual = (token_rows.astype(jnp.float32) + attn_total).astype(jnp.bfloat16)
        mlp_in = rms_norm(residual.astype(jnp.float32), mlp_gain).astype(jnp.bfloat16)
        gate = jnp.dot(mlp_in, gate_weight, preferred_element_type=jnp.float32)
        upward = jnp.dot(mlp_in, up_weight, preferred_element_type=jnp.float32)
        hidden = (jax.nn.gelu(gate, approximate=True) * upward).astype(jnp.bfloat16)
        mlp_part = jnp.dot(hidden, down_weight, preferred_element_type=jnp.float32).astype(
            jnp.bfloat16
        )
        mlp_total = tree_sum(mlp_part, "tp", tp_size).astype(jnp.float32)
        layer_out = (residual.astype(jnp.float32) + mlp_total).astype(jnp.bfloat16)
        return layer_out.reshape(req_dev, steps, width)

    return body


def solution(mesh):
    return jax.shard_map(
        make_body(mesh.shape["req"], mesh.shape["tp"]),
        mesh=mesh,
        in_specs=(
            P("req", None, None),
            P("req"),
            P("req", None),
            P("req", None, None, None),
            P(),
            P(None, "tp"),
            P(),
            P(),
            P("tp", None),
            P(),
            P(None, "tp"),
            P(None, "tp"),
            P("tp", None),
        ),
        out_specs=P("req", None, None),
        check_vma=False,
    )
```

```python
import jax
import jax.numpy as jnp
from jax import lax
from jax.sharding import PartitionSpec as P

WINDOW = 1024


negative = -1e30
epsilon = 1e-06


def rms_norm(values, gain):
    return values * lax.rsqrt(jnp.mean(values * values, axis=-1, keepdims=True) + epsilon) * gain


def tree_sum(values, axis, size):
    step = 1
    while step < size:
        values = values + lax.ppermute(values, axis, [(i, i ^ step) for i in range(size)])
        step *= 2
    return values


def tree_gather(values, axis, size):
    index = lax.axis_index(axis)
    parts = values[None]
    step = 1
    while step < size:
        other = lax.ppermute(parts, axis, [(i, i ^ step) for i in range(size)])
        upper = (index // step) % 2 == 1
        parts = jnp.concatenate(
            [jnp.where(upper, other, parts), jnp.where(upper, parts, other)], axis=0
        )
        step *= 2
    return parts


def make_body(req_size, tp_size):
    def body(
        tokens,
        lengths,
        page_table,
        kv_pages,
        norm_gain,
        query_weight,
        key_weight,
        value_weight,
        out_weight,
        mlp_gain,
        gate_weight,
        up_weight,
        down_weight,
    ):
        req_dev, steps, width = tokens.shape
        head_dim = key_weight.shape[1]
        heads_dev = query_weight.shape[1] // head_dim
        pool_size = kv_pages.shape[0]
        page_size = kv_pages.shape[2]
        window_pages = page_table.shape[1]
        requests = req_dev * req_size
        qwidth = steps * heads_dev * head_dim
        token_rows = tokens.reshape(req_dev * steps, width)
        normed = rms_norm(token_rows.astype(jnp.float32), norm_gain).astype(jnp.bfloat16)
        queries = (
            jnp.dot(normed, query_weight, preferred_element_type=jnp.float32) * head_dim ** (-0.5)
        ).astype(jnp.bfloat16)
        key_new = jnp.dot(normed, key_weight, preferred_element_type=jnp.float32).astype(jnp.bfloat16)
        value_new = jnp.dot(normed, value_weight, preferred_element_type=jnp.float32).astype(
            jnp.bfloat16
        )
        ints = jnp.concatenate([page_table, lengths.reshape(req_dev, 1)], axis=1)
        packed = jnp.concatenate(
            [
                queries.reshape(req_dev, qwidth),
                (ints // 256).astype(jnp.bfloat16),
                (ints % 256).astype(jnp.bfloat16),
            ],
            axis=1,
        )
        gathered = lax.all_to_all(
            jnp.broadcast_to(packed[None], (req_size,) + packed.shape), "req", 0, 0, tiled=False
        ).reshape(requests, packed.shape[1])
        all_queries = gathered[:, :qwidth].reshape(requests, steps * heads_dev, head_dim)
        nints = window_pages + 1
        digits = gathered[:, qwidth:].astype(jnp.int32)
        all_ints = digits[:, :nints] * 256 + digits[:, nints:]
        all_table = all_ints[:, :window_pages]
        all_lengths = all_ints[:, window_pages]
        flat_table = all_table.reshape(-1)
        entries = flat_table.shape[0]
        my_slots = lax.axis_index("req") * pool_size + jnp.arange(pool_size, dtype=jnp.int32)
        match = flat_table[None, :] == my_slots[:, None]
        owner_entry = jnp.sum(
            jnp.where(match, jnp.arange(entries, dtype=jnp.int32)[None, :], 0), axis=1
        )
        page_request = owner_entry // window_pages
        page_number = owner_entry % window_pages
        page_length = all_lengths[page_request]
        first_page = jnp.maximum(page_length - (WINDOW - 1), 0) // page_size
        position = (first_page + page_number)[:, None] * page_size + jnp.arange(
            page_size, dtype=jnp.int32
        )[None, :]
        current = page_length[:, None] + jnp.arange(steps, dtype=jnp.int32)[None, :]
        visible = (position[:, None, :] < page_length[:, None, None]) & (
            position[:, None, :] > current[:, :, None] - WINDOW
        )
        visible = visible[:, :, None, :]
        page_queries = all_queries[page_request]
        scores = jnp.einsum(
            "pqd,pkd->pqk", page_queries, kv_pages[:, 0], preferred_element_type=jnp.float32
        )
        scores = jnp.where(visible, scores.reshape(pool_size, steps, heads_dev, page_size), negative)
        block_max = jnp.max(scores, axis=-1)
        weights = jnp.where(visible, jnp.exp(scores - block_max[..., None]), 0.0)
        block_total = jnp.sum(weights, axis=-1)
        block_out = jnp.einsum(
            "pqk,pkd->pqd",
            weights.astype(jnp.bfloat16).reshape(pool_size, steps * heads_dev, page_size),
            kv_pages[:, 1],
            preferred_element_type=jnp.float32,
        )
        block_out = block_out.reshape(pool_size, steps, heads_dev, head_dim)
        member = page_request[None, :] == jnp.arange(requests, dtype=jnp.int32)[:, None]
        local_max = jnp.max(
            jnp.where(member[:, :, None, None], block_max[None], negative), axis=1
        )
        scale = jnp.exp(block_max - local_max[page_request])
        nsh = steps * heads_dev
        scaled = jnp.concatenate(
            [
                (block_out * scale[..., None]).reshape(pool_size, nsh * head_dim),
                (block_total * scale).reshape(pool_size, nsh),
            ],
            axis=1,
        )
        sent = jnp.dot(
            member.astype(jnp.float32),
            scaled,
            precision=lax.Precision.HIGHEST,
            preferred_element_type=jnp.float32,
        )
        send = jnp.concatenate([sent, local_max.reshape(requests, nsh)], axis=1)
        recv = lax.all_to_all(send, "req", 0, 0, tiled=True).reshape(req_size, req_dev, -1)
        got_out = recv[:, :, : nsh * head_dim].reshape(req_size, req_dev, steps, heads_dev, head_dim)
        got_total = recv[:, :, nsh * head_dim : nsh * (head_dim + 1)].reshape(
            req_size, req_dev, steps, heads_dev
        )
        got_max = recv[:, :, nsh * (head_dim + 1) :].reshape(req_size, req_dev, steps, heads_dev)
        cache_max = jnp.max(got_max, axis=0)
        local_queries = queries.reshape(req_dev, steps, heads_dev, head_dim)
        new_scores = jnp.einsum(
            "rshd,rtd->rsht",
            local_queries,
            key_new.reshape(req_dev, steps, head_dim),
            preferred_element_type=jnp.float32,
        )
        causal = (jnp.arange(steps)[None, :] <= jnp.arange(steps)[:, None])[None, :, None, :]
        new_scores = jnp.where(causal, new_scores, negative)
        new_max = jnp.max(new_scores, axis=-1)
        new_weights = jnp.where(causal, jnp.exp(new_scores - new_max[..., None]), 0.0)
        new_total = jnp.sum(new_weights, axis=-1)
        new_out = jnp.einsum(
            "rsht,rtd->rshd",
            new_weights.astype(jnp.bfloat16),
            value_new.reshape(req_dev, steps, head_dim),
            preferred_element_type=jnp.float32,
        )
        overall = jnp.maximum(cache_max, new_max)
        src_scale = jnp.exp(got_max - overall[None])
        new_scale = jnp.exp(new_max - overall)
        total = jnp.sum(got_total * src_scale, axis=0) + new_total * new_scale
        summed = jnp.sum(got_out * src_scale[..., None], axis=0) + new_out * new_scale[..., None]
        attended = (
            (summed / total[..., None])
            .astype(jnp.bfloat16)
            .reshape(req_dev * steps, heads_dev * head_dim)
        )
        projected = jnp.dot(attended, out_weight, preferred_element_type=jnp.float32)
        attn_total = tree_sum(projected.astype(jnp.bfloat16), "tp", tp_size).astype(jnp.float32)
        residual = (token_rows.astype(jnp.float32) + attn_total).astype(jnp.bfloat16)
        mlp_in = rms_norm(residual.astype(jnp.float32), mlp_gain).astype(jnp.bfloat16)
        gate = jnp.dot(mlp_in, gate_weight, preferred_element_type=jnp.float32)
        upward = jnp.dot(mlp_in, up_weight, preferred_element_type=jnp.float32)
        hidden = (jax.nn.gelu(gate, approximate=True) * upward).astype(jnp.bfloat16)
        mlp_part = jnp.dot(hidden, down_weight, preferred_element_type=jnp.float32).astype(
            jnp.bfloat16
        )
        mlp_total = tree_sum(mlp_part, "tp", tp_size).astype(jnp.float32)
        layer_out = (residual.astype(jnp.float32) + mlp_total).astype(jnp.bfloat16)
        return layer_out.reshape(req_dev, steps, width)

    return body


def solution(mesh):
    return jax.shard_map(
        make_body(mesh.shape["req"], mesh.shape["tp"]),
        mesh=mesh,
        in_specs=(
            P("req", None, None),
            P("req"),
            P("req", None),
            P("req", None, None, None),
            P(),
            P(None, "tp"),
            P(),
            P(),
            P("tp", None),
            P(),
            P(None, "tp"),
            P(None, "tp"),
            P("tp", None),
        ),
        out_specs=P("req", None, None),
        check_vma=False,
    )
```

```python
import jax
import jax.numpy as jnp
from jax import lax
from jax.sharding import PartitionSpec as P

WINDOW = 1024


negative = -1e30
epsilon = 1e-06


def rms_norm(values, gain):
    return values * lax.rsqrt(jnp.mean(values * values, axis=-1, keepdims=True) + epsilon) * gain


def tree_sum(values, axis, size):
    step = 1
    while step < size:
        values = values + lax.ppermute(values, axis, [(i, i ^ step) for i in range(size)])
        step *= 2
    return values


def tree_gather(values, axis, size):
    index = lax.axis_index(axis)
    parts = values[None]
    step = 1
    while step < size:
        other = lax.ppermute(parts, axis, [(i, i ^ step) for i in range(size)])
        upper = (index // step) % 2 == 1
        parts = jnp.concatenate(
            [jnp.where(upper, other, parts), jnp.where(upper, parts, other)], axis=0
        )
        step *= 2
    return parts


def make_body(req_size, tp_size):
    def body(
        tokens,
        lengths,
        page_table,
        kv_pages,
        norm_gain,
        query_weight,
        key_weight,
        value_weight,
        out_weight,
        mlp_gain,
        gate_weight,
        up_weight,
        down_weight,
    ):
        req_dev, steps, width = tokens.shape
        head_dim = key_weight.shape[1]
        heads_dev = query_weight.shape[1] // head_dim
        pool_size = kv_pages.shape[0]
        page_size = kv_pages.shape[2]
        window_pages = page_table.shape[1]
        requests = req_dev * req_size
        qwidth = steps * heads_dev * head_dim
        token_rows = tokens.reshape(req_dev * steps, width)
        normed = rms_norm(token_rows.astype(jnp.float32), norm_gain).astype(jnp.bfloat16)
        queries = (
            jnp.dot(normed, query_weight, preferred_element_type=jnp.float32) * head_dim ** (-0.5)
        ).astype(jnp.bfloat16)
        key_new = jnp.dot(normed, key_weight, preferred_element_type=jnp.float32).astype(jnp.bfloat16)
        value_new = jnp.dot(normed, value_weight, preferred_element_type=jnp.float32).astype(
            jnp.bfloat16
        )
        ints = jnp.concatenate([page_table, lengths.reshape(req_dev, 1)], axis=1)
        packed = jnp.concatenate(
            [
                queries.reshape(req_dev, qwidth),
                (ints // 256).astype(jnp.bfloat16),
                (ints % 256).astype(jnp.bfloat16),
            ],
            axis=1,
        )
        gathered = lax.all_to_all(
            jnp.broadcast_to(packed[None], (req_size,) + packed.shape), "req", 0, 0, tiled=False
        ).reshape(requests, packed.shape[1])
        all_queries = gathered[:, :qwidth].reshape(requests, steps * heads_dev, head_dim)
        nints = window_pages + 1
        digits = gathered[:, qwidth:].astype(jnp.int32)
        all_ints = digits[:, :nints] * 256 + digits[:, nints:]
        all_table = all_ints[:, :window_pages]
        all_lengths = all_ints[:, window_pages]
        flat_table = all_table.reshape(-1)
        entries = flat_table.shape[0]
        my_slots = lax.axis_index("req") * pool_size + jnp.arange(pool_size, dtype=jnp.int32)
        match = flat_table[None, :] == my_slots[:, None]
        owner_entry = jnp.sum(
            jnp.where(match, jnp.arange(entries, dtype=jnp.int32)[None, :], 0), axis=1
        )
        page_request = owner_entry // window_pages
        page_number = owner_entry % window_pages
        page_length = all_lengths[page_request]
        first_page = jnp.maximum(page_length - (WINDOW - 1), 0) // page_size
        position = (first_page + page_number)[:, None] * page_size + jnp.arange(
            page_size, dtype=jnp.int32
        )[None, :]
        current = page_length[:, None] + jnp.arange(steps, dtype=jnp.int32)[None, :]
        visible = (position[:, None, :] < page_length[:, None, None]) & (
            position[:, None, :] > current[:, :, None] - WINDOW
        )
        visible = visible[:, :, None, :]
        page_queries = all_queries[page_request]
        scores = jnp.einsum(
            "pqd,pkd->pqk", page_queries, kv_pages[:, 0], preferred_element_type=jnp.float32
        )
        scores = jnp.where(visible, scores.reshape(pool_size, steps, heads_dev, page_size), negative)
        block_max = jnp.max(scores, axis=-1)
        weights = jnp.where(visible, jnp.exp(scores - block_max[..., None]), 0.0)
        block_total = jnp.sum(weights, axis=-1)
        block_out = jnp.einsum(
            "pqk,pkd->pqd",
            weights.astype(jnp.bfloat16).reshape(pool_size, steps * heads_dev, page_size),
            kv_pages[:, 1],
            preferred_element_type=jnp.float32,
        )
        block_out = block_out.reshape(pool_size, steps, heads_dev, head_dim)
        member = page_request[None, :] == jnp.arange(requests, dtype=jnp.int32)[:, None]
        local_max = jnp.max(
            jnp.where(member[:, :, None, None], block_max[None], negative), axis=1
        )
        scale = jnp.exp(block_max - local_max[page_request])
        nsh = steps * heads_dev
        scaled = jnp.concatenate(
            [
                (block_out * scale[..., None]).reshape(pool_size, nsh * head_dim),
                (block_total * scale).reshape(pool_size, nsh),
            ],
            axis=1,
        )
        sent = jnp.dot(
            member.astype(jnp.float32),
            scaled,
            precision=lax.Precision.HIGHEST,
            preferred_element_type=jnp.float32,
        )
        flat_max = local_max.reshape(requests, nsh)
        max_hi = lax.reduce_precision(flat_max, exponent_bits=8, mantissa_bits=7)
        rest = flat_max - max_hi
        max_mid = lax.reduce_precision(rest, exponent_bits=8, mantissa_bits=7)
        max_lo = rest - max_mid
        send = jnp.concatenate(
            [sent, max_hi, max_mid, max_lo], axis=1
        ).astype(jnp.bfloat16)
        recv = lax.all_to_all(send, "req", 0, 0, tiled=True).reshape(req_size, req_dev, -1)
        got_out = (
            recv[:, :, : nsh * head_dim]
            .astype(jnp.float32)
            .reshape(req_size, req_dev, steps, heads_dev, head_dim)
        )
        got_total = (
            recv[:, :, nsh * head_dim : nsh * (head_dim + 1)]
            .astype(jnp.float32)
            .reshape(req_size, req_dev, steps, heads_dev)
        )
        pieces = recv[:, :, nsh * (head_dim + 1) :].astype(jnp.float32)
        got_max = (
            (pieces[:, :, :nsh] + pieces[:, :, nsh : 2 * nsh]) + pieces[:, :, 2 * nsh :]
        ).reshape(req_size, req_dev, steps, heads_dev)
        cache_max = jnp.max(got_max, axis=0)
        local_queries = queries.reshape(req_dev, steps, heads_dev, head_dim)
        new_scores = jnp.einsum(
            "rshd,rtd->rsht",
            local_queries,
            key_new.reshape(req_dev, steps, head_dim),
            preferred_element_type=jnp.float32,
        )
        causal = (jnp.arange(steps)[None, :] <= jnp.arange(steps)[:, None])[None, :, None, :]
        new_scores = jnp.where(causal, new_scores, negative)
        new_max = jnp.max(new_scores, axis=-1)
        new_weights = jnp.where(causal, jnp.exp(new_scores - new_max[..., None]), 0.0)
        new_total = jnp.sum(new_weights, axis=-1)
        new_out = jnp.einsum(
            "rsht,rtd->rshd",
            new_weights.astype(jnp.bfloat16),
            value_new.reshape(req_dev, steps, head_dim),
            preferred_element_type=jnp.float32,
        )
        overall = jnp.maximum(cache_max, new_max)
        src_scale = jnp.exp(got_max - overall[None])
        new_scale = jnp.exp(new_max - overall)
        total = jnp.sum(got_total * src_scale, axis=0) + new_total * new_scale
        summed = jnp.sum(got_out * src_scale[..., None], axis=0) + new_out * new_scale[..., None]
        attended = (
            (summed / total[..., None])
            .astype(jnp.bfloat16)
            .reshape(req_dev * steps, heads_dev * head_dim)
        )
        projected = jnp.dot(attended, out_weight, preferred_element_type=jnp.float32)
        attn_total = tree_sum(projected.astype(jnp.bfloat16), "tp", tp_size).astype(jnp.float32)
        residual = (token_rows.astype(jnp.float32) + attn_total).astype(jnp.bfloat16)
        mlp_in = rms_norm(residual.astype(jnp.float32), mlp_gain).astype(jnp.bfloat16)
        gate = jnp.dot(mlp_in, gate_weight, preferred_element_type=jnp.float32)
        upward = jnp.dot(mlp_in, up_weight, preferred_element_type=jnp.float32)
        hidden = (jax.nn.gelu(gate, approximate=True) * upward).astype(jnp.bfloat16)
        mlp_part = jnp.dot(hidden, down_weight, preferred_element_type=jnp.float32).astype(
            jnp.bfloat16
        )
        mlp_total = tree_sum(mlp_part, "tp", tp_size).astype(jnp.float32)
        layer_out = (residual.astype(jnp.float32) + mlp_total).astype(jnp.bfloat16)
        return layer_out.reshape(req_dev, steps, width)

    return body


def solution(mesh):
    return jax.shard_map(
        make_body(mesh.shape["req"], mesh.shape["tp"]),
        mesh=mesh,
        in_specs=(
            P("req", None, None),
            P("req"),
            P("req", None),
            P("req", None, None, None),
            P(),
            P(None, "tp"),
            P(),
            P(),
            P("tp", None),
            P(),
            P(None, "tp"),
            P(None, "tp"),
            P("tp", None),
        ),
        out_specs=P("req", None, None),
        check_vma=False,
    )
```

```python
import jax
import jax.numpy as jnp
from jax import lax
from jax.sharding import PartitionSpec as P

WINDOW = 1024


negative = -1e30
epsilon = 1e-06


def rms_norm(values, gain):
    return values * lax.rsqrt(jnp.mean(values * values, axis=-1, keepdims=True) + epsilon) * gain


def staggered_sum(values, req_size, tp_size):
    steps = []
    step = 1
    while step < tp_size:
        steps.append(step)
        step *= 2
    for round_index in range(len(steps)):
        pairs = []
        for q in range(req_size):
            order = steps if q % 2 == 0 else steps[::-1]
            for t in range(tp_size):
                pairs.append((q * tp_size + t, q * tp_size + (t ^ order[round_index])))
        values = values + lax.ppermute(values, ("req", "tp"), pairs)
    return values


def make_body(req_size, tp_size):
    def body(
        tokens,
        lengths,
        page_table,
        kv_pages,
        norm_gain,
        query_weight,
        key_weight,
        value_weight,
        out_weight,
        mlp_gain,
        gate_weight,
        up_weight,
        down_weight,
    ):
        req_dev, steps, width = tokens.shape
        head_dim = key_weight.shape[1]
        heads_dev = query_weight.shape[1] // head_dim
        pool_size = kv_pages.shape[0]
        page_size = kv_pages.shape[2]
        window_pages = page_table.shape[1]
        requests = req_dev * req_size
        qwidth = steps * heads_dev * head_dim
        token_rows = tokens.reshape(req_dev * steps, width)
        normed = rms_norm(token_rows.astype(jnp.float32), norm_gain).astype(jnp.bfloat16)
        queries = (
            jnp.dot(normed, query_weight, preferred_element_type=jnp.float32) * head_dim ** (-0.5)
        ).astype(jnp.bfloat16)
        key_new = jnp.dot(normed, key_weight, preferred_element_type=jnp.float32).astype(jnp.bfloat16)
        value_new = jnp.dot(normed, value_weight, preferred_element_type=jnp.float32).astype(
            jnp.bfloat16
        )
        ints = jnp.concatenate([page_table, lengths.reshape(req_dev, 1)], axis=1)
        packed = jnp.concatenate(
            [
                queries.reshape(req_dev, qwidth),
                (ints // 256).astype(jnp.bfloat16),
                (ints % 256).astype(jnp.bfloat16),
            ],
            axis=1,
        )
        gathered = lax.all_to_all(
            jnp.broadcast_to(packed[None], (req_size,) + packed.shape), "req", 0, 0, tiled=False
        ).reshape(requests, packed.shape[1])
        all_queries = gathered[:, :qwidth].reshape(requests, steps * heads_dev, head_dim)
        nints = window_pages + 1
        digits = gathered[:, qwidth:].astype(jnp.int32)
        all_ints = digits[:, :nints] * 256 + digits[:, nints:]
        all_table = all_ints[:, :window_pages]
        all_lengths = all_ints[:, window_pages]
        flat_table = all_table.reshape(-1)
        entries = flat_table.shape[0]
        my_slots = lax.axis_index("req") * pool_size + jnp.arange(pool_size, dtype=jnp.int32)
        match = flat_table[None, :] == my_slots[:, None]
        owner_entry = jnp.sum(
            jnp.where(match, jnp.arange(entries, dtype=jnp.int32)[None, :], 0), axis=1
        )
        page_request = owner_entry // window_pages
        page_number = owner_entry % window_pages
        page_length = all_lengths[page_request]
        first_page = jnp.maximum(page_length - (WINDOW - 1), 0) // page_size
        position = (first_page + page_number)[:, None] * page_size + jnp.arange(
            page_size, dtype=jnp.int32
        )[None, :]
        current = page_length[:, None] + jnp.arange(steps, dtype=jnp.int32)[None, :]
        visible = (position[:, None, :] < page_length[:, None, None]) & (
            position[:, None, :] > current[:, :, None] - WINDOW
        )
        visible = visible[:, :, None, :]
        page_queries = all_queries[page_request]
        scores = jnp.einsum(
            "pqd,pkd->pqk", page_queries, kv_pages[:, 0], preferred_element_type=jnp.float32
        )
        scores = jnp.where(visible, scores.reshape(pool_size, steps, heads_dev, page_size), negative)
        block_max = jnp.max(scores, axis=-1)
        weights = jnp.where(visible, jnp.exp(scores - block_max[..., None]), 0.0)
        block_total = jnp.sum(weights, axis=-1)
        block_out = jnp.einsum(
            "pqk,pkd->pqd",
            weights.astype(jnp.bfloat16).reshape(pool_size, steps * heads_dev, page_size),
            kv_pages[:, 1],
            preferred_element_type=jnp.float32,
        )
        block_out = block_out.reshape(pool_size, steps, heads_dev, head_dim)
        member = page_request[None, :] == jnp.arange(requests, dtype=jnp.int32)[:, None]
        local_max = jnp.max(
            jnp.where(member[:, :, None, None], block_max[None], negative), axis=1
        )
        scale = jnp.exp(block_max - local_max[page_request])
        nsh = steps * heads_dev
        scaled = jnp.concatenate(
            [
                (block_out * scale[..., None]).reshape(pool_size, nsh * head_dim),
                (block_total * scale).reshape(pool_size, nsh),
            ],
            axis=1,
        )
        sent = jnp.dot(
            member.astype(jnp.float32),
            scaled,
            precision=lax.Precision.HIGHEST,
            preferred_element_type=jnp.float32,
        )
        flat_max = local_max.reshape(requests, nsh)
        max_hi = lax.reduce_precision(flat_max, exponent_bits=8, mantissa_bits=7)
        rest = flat_max - max_hi
        max_mid = lax.reduce_precision(rest, exponent_bits=8, mantissa_bits=7)
        max_lo = rest - max_mid
        send = jnp.concatenate(
            [sent, max_hi, max_mid, max_lo], axis=1
        ).astype(jnp.bfloat16)
        recv = lax.all_to_all(send, "req", 0, 0, tiled=True).reshape(req_size, req_dev, -1)
        got_out = (
            recv[:, :, : nsh * head_dim]
            .astype(jnp.float32)
            .reshape(req_size, req_dev, steps, heads_dev, head_dim)
        )
        got_total = (
            recv[:, :, nsh * head_dim : nsh * (head_dim + 1)]
            .astype(jnp.float32)
            .reshape(req_size, req_dev, steps, heads_dev)
        )
        pieces = recv[:, :, nsh * (head_dim + 1) :].astype(jnp.float32)
        got_max = (
            (pieces[:, :, :nsh] + pieces[:, :, nsh : 2 * nsh]) + pieces[:, :, 2 * nsh :]
        ).reshape(req_size, req_dev, steps, heads_dev)
        cache_max = jnp.max(got_max, axis=0)
        local_queries = queries.reshape(req_dev, steps, heads_dev, head_dim)
        new_scores = jnp.einsum(
            "rshd,rtd->rsht",
            local_queries,
            key_new.reshape(req_dev, steps, head_dim),
            preferred_element_type=jnp.float32,
        )
        causal = (jnp.arange(steps)[None, :] <= jnp.arange(steps)[:, None])[None, :, None, :]
        new_scores = jnp.where(causal, new_scores, negative)
        new_max = jnp.max(new_scores, axis=-1)
        new_weights = jnp.where(causal, jnp.exp(new_scores - new_max[..., None]), 0.0)
        new_total = jnp.sum(new_weights, axis=-1)
        new_out = jnp.einsum(
            "rsht,rtd->rshd",
            new_weights.astype(jnp.bfloat16),
            value_new.reshape(req_dev, steps, head_dim),
            preferred_element_type=jnp.float32,
        )
        overall = jnp.maximum(cache_max, new_max)
        src_scale = jnp.exp(got_max - overall[None])
        new_scale = jnp.exp(new_max - overall)
        total = jnp.sum(got_total * src_scale, axis=0) + new_total * new_scale
        summed = jnp.sum(got_out * src_scale[..., None], axis=0) + new_out * new_scale[..., None]
        attended = (
            (summed / total[..., None])
            .astype(jnp.bfloat16)
            .reshape(req_dev * steps, heads_dev * head_dim)
        )
        projected = jnp.dot(attended, out_weight, preferred_element_type=jnp.float32)
        attn_total = staggered_sum(projected.astype(jnp.bfloat16), req_size, tp_size).astype(jnp.float32)
        residual = (token_rows.astype(jnp.float32) + attn_total).astype(jnp.bfloat16)
        mlp_in = rms_norm(residual.astype(jnp.float32), mlp_gain).astype(jnp.bfloat16)
        gate = jnp.dot(mlp_in, gate_weight, preferred_element_type=jnp.float32)
        upward = jnp.dot(mlp_in, up_weight, preferred_element_type=jnp.float32)
        hidden = (jax.nn.gelu(gate, approximate=True) * upward).astype(jnp.bfloat16)
        mlp_part = jnp.dot(hidden, down_weight, preferred_element_type=jnp.float32).astype(
            jnp.bfloat16
        )
        mlp_total = staggered_sum(mlp_part, req_size, tp_size).astype(jnp.float32)
        layer_out = (residual.astype(jnp.float32) + mlp_total).astype(jnp.bfloat16)
        return layer_out.reshape(req_dev, steps, width)

    return body


def solution(mesh):
    return jax.shard_map(
        make_body(mesh.shape["req"], mesh.shape["tp"]),
        mesh=mesh,
        in_specs=(
            P("req", None, None),
            P("req"),
            P("req", None),
            P("req", None, None, None),
            P(),
            P(None, "tp"),
            P(),
            P(),
            P("tp", None),
            P(),
            P(None, "tp"),
            P(None, "tp"),
            P("tp", None),
        ),
        out_specs=P("req", None, None),
        check_vma=False,
    )
```

```python
import jax
import jax.numpy as jnp
from jax import lax
from jax.sharding import PartitionSpec as P

WINDOW = 1024


negative = -1e30
epsilon = 1e-06


def rms_norm(values, gain):
    return values * lax.rsqrt(jnp.mean(values * values, axis=-1, keepdims=True) + epsilon) * gain


def staggered_sum(values, req_size, tp_size):
    steps = []
    step = 1
    while step < tp_size:
        steps.append(step)
        step *= 2
    for round_index in range(len(steps)):
        pairs = []
        for q in range(req_size):
            order = steps if q % 2 == 0 else steps[::-1]
            for t in range(tp_size):
                pairs.append((q * tp_size + t, q * tp_size + (t ^ order[round_index])))
        values = values + lax.ppermute(values, ("req", "tp"), pairs)
    return values


def tree_gather(values, axis, size):
    index = lax.axis_index(axis)
    parts = values[None]
    step = 1
    while step < size:
        other = lax.ppermute(parts, axis, [(i, i ^ step) for i in range(size)])
        upper = (index // step) % 2 == 1
        parts = jnp.concatenate(
            [jnp.where(upper, other, parts), jnp.where(upper, parts, other)], axis=0
        )
        step *= 2
    return parts


def make_body(req_size, tp_size):
    def body(
        tokens,
        lengths,
        page_table,
        kv_pages,
        norm_gain,
        query_weight,
        key_weight,
        value_weight,
        out_weight,
        mlp_gain,
        gate_weight,
        up_weight,
        down_weight,
    ):
        req_dev, steps, width = tokens.shape
        head_dim = key_weight.shape[1]
        heads_dev = query_weight.shape[1] // head_dim
        pool_size = kv_pages.shape[0]
        page_size = kv_pages.shape[2]
        window_pages = page_table.shape[1]
        requests = req_dev * req_size
        qwidth = steps * heads_dev * head_dim
        token_rows = tokens.reshape(req_dev * steps, width)
        full_out_weight = lax.all_to_all(
            jnp.broadcast_to(out_weight[None], (tp_size,) + out_weight.shape), "tp", 0, 0, tiled=False
        ).reshape(tp_size * out_weight.shape[0], width)
        normed = rms_norm(token_rows.astype(jnp.float32), norm_gain).astype(jnp.bfloat16)
        queries = (
            jnp.dot(normed, query_weight, preferred_element_type=jnp.float32) * head_dim ** (-0.5)
        ).astype(jnp.bfloat16)
        key_new = jnp.dot(normed, key_weight, preferred_element_type=jnp.float32).astype(jnp.bfloat16)
        value_new = jnp.dot(normed, value_weight, preferred_element_type=jnp.float32).astype(
            jnp.bfloat16
        )
        ints = jnp.concatenate([page_table, lengths.reshape(req_dev, 1)], axis=1)
        packed = jnp.concatenate(
            [
                queries.reshape(req_dev, qwidth),
                (ints // 256).astype(jnp.bfloat16),
                (ints % 256).astype(jnp.bfloat16),
            ],
            axis=1,
        )
        gathered = lax.all_to_all(
            jnp.broadcast_to(packed[None], (req_size,) + packed.shape), "req", 0, 0, tiled=False
        ).reshape(requests, packed.shape[1])
        all_queries = gathered[:, :qwidth].reshape(requests, steps * heads_dev, head_dim)
        nints = window_pages + 1
        digits = gathered[:, qwidth:].astype(jnp.int32)
        all_ints = digits[:, :nints] * 256 + digits[:, nints:]
        all_table = all_ints[:, :window_pages]
        all_lengths = all_ints[:, window_pages]
        flat_table = all_table.reshape(-1)
        entries = flat_table.shape[0]
        my_slots = lax.axis_index("req") * pool_size + jnp.arange(pool_size, dtype=jnp.int32)
        match = flat_table[None, :] == my_slots[:, None]
        owner_entry = jnp.sum(
            jnp.where(match, jnp.arange(entries, dtype=jnp.int32)[None, :], 0), axis=1
        )
        page_request = owner_entry // window_pages
        page_number = owner_entry % window_pages
        page_length = all_lengths[page_request]
        first_page = jnp.maximum(page_length - (WINDOW - 1), 0) // page_size
        position = (first_page + page_number)[:, None] * page_size + jnp.arange(
            page_size, dtype=jnp.int32
        )[None, :]
        current = page_length[:, None] + jnp.arange(steps, dtype=jnp.int32)[None, :]
        visible = (position[:, None, :] < page_length[:, None, None]) & (
            position[:, None, :] > current[:, :, None] - WINDOW
        )
        visible = visible[:, :, None, :]
        page_queries = all_queries[page_request]
        scores = jnp.einsum(
            "pqd,pkd->pqk", page_queries, kv_pages[:, 0], preferred_element_type=jnp.float32
        )
        scores = jnp.where(visible, scores.reshape(pool_size, steps, heads_dev, page_size), negative)
        block_max = jnp.max(scores, axis=-1)
        weights = jnp.where(visible, jnp.exp(scores - block_max[..., None]), 0.0)
        block_total = jnp.sum(weights, axis=-1)
        block_out = jnp.einsum(
            "pqk,pkd->pqd",
            weights.astype(jnp.bfloat16).reshape(pool_size, steps * heads_dev, page_size),
            kv_pages[:, 1],
            preferred_element_type=jnp.float32,
        )
        block_out = block_out.reshape(pool_size, steps, heads_dev, head_dim)
        member = page_request[None, :] == jnp.arange(requests, dtype=jnp.int32)[:, None]
        local_max = jnp.max(
            jnp.where(member[:, :, None, None], block_max[None], negative), axis=1
        )
        scale = jnp.exp(block_max - local_max[page_request])
        nsh = steps * heads_dev
        scaled = jnp.concatenate(
            [
                (block_out * scale[..., None]).reshape(pool_size, nsh * head_dim),
                (block_total * scale).reshape(pool_size, nsh),
            ],
            axis=1,
        )
        sent = jnp.dot(
            member.astype(jnp.float32),
            scaled,
            precision=lax.Precision.HIGHEST,
            preferred_element_type=jnp.float32,
        )
        flat_max = local_max.reshape(requests, nsh)
        max_hi = lax.reduce_precision(flat_max, exponent_bits=8, mantissa_bits=7)
        rest = flat_max - max_hi
        max_mid = lax.reduce_precision(rest, exponent_bits=8, mantissa_bits=7)
        max_lo = rest - max_mid
        send = jnp.concatenate(
            [sent, max_hi, max_mid, max_lo], axis=1
        ).astype(jnp.bfloat16)
        recv = lax.all_to_all(send, "req", 0, 0, tiled=True).reshape(req_size, req_dev, -1)
        got_out = (
            recv[:, :, : nsh * head_dim]
            .astype(jnp.float32)
            .reshape(req_size, req_dev, steps, heads_dev, head_dim)
        )
        got_total = (
            recv[:, :, nsh * head_dim : nsh * (head_dim + 1)]
            .astype(jnp.float32)
            .reshape(req_size, req_dev, steps, heads_dev)
        )
        pieces = recv[:, :, nsh * (head_dim + 1) :].astype(jnp.float32)
        got_max = (
            (pieces[:, :, :nsh] + pieces[:, :, nsh : 2 * nsh]) + pieces[:, :, 2 * nsh :]
        ).reshape(req_size, req_dev, steps, heads_dev)
        cache_max = jnp.max(got_max, axis=0)
        local_queries = queries.reshape(req_dev, steps, heads_dev, head_dim)
        new_scores = jnp.einsum(
            "rshd,rtd->rsht",
            local_queries,
            key_new.reshape(req_dev, steps, head_dim),
            preferred_element_type=jnp.float32,
        )
        causal = (jnp.arange(steps)[None, :] <= jnp.arange(steps)[:, None])[None, :, None, :]
        new_scores = jnp.where(causal, new_scores, negative)
        new_max = jnp.max(new_scores, axis=-1)
        new_weights = jnp.where(causal, jnp.exp(new_scores - new_max[..., None]), 0.0)
        new_total = jnp.sum(new_weights, axis=-1)
        new_out = jnp.einsum(
            "rsht,rtd->rshd",
            new_weights.astype(jnp.bfloat16),
            value_new.reshape(req_dev, steps, head_dim),
            preferred_element_type=jnp.float32,
        )
        overall = jnp.maximum(cache_max, new_max)
        src_scale = jnp.exp(got_max - overall[None])
        new_scale = jnp.exp(new_max - overall)
        total = jnp.sum(got_total * src_scale, axis=0) + new_total * new_scale
        summed = jnp.sum(got_out * src_scale[..., None], axis=0) + new_out * new_scale[..., None]
        attended = (
            (summed / total[..., None])
            .astype(jnp.bfloat16)
            .reshape(req_dev * steps, heads_dev * head_dim)
        )
        all_heads = tree_gather(attended, "tp", tp_size)
        all_heads = jnp.moveaxis(all_heads, 0, 1).reshape(req_dev * steps, -1)
        attn_total = jnp.dot(all_heads, full_out_weight, preferred_element_type=jnp.float32)
        residual = (token_rows.astype(jnp.float32) + attn_total).astype(jnp.bfloat16)
        mlp_in = rms_norm(residual.astype(jnp.float32), mlp_gain).astype(jnp.bfloat16)
        gate = jnp.dot(mlp_in, gate_weight, preferred_element_type=jnp.float32)
        upward = jnp.dot(mlp_in, up_weight, preferred_element_type=jnp.float32)
        hidden = (jax.nn.gelu(gate, approximate=True) * upward).astype(jnp.bfloat16)
        mlp_part = jnp.dot(hidden, down_weight, preferred_element_type=jnp.float32).astype(
            jnp.bfloat16
        )
        mlp_total = staggered_sum(mlp_part, req_size, tp_size).astype(jnp.float32)
        layer_out = (residual.astype(jnp.float32) + mlp_total).astype(jnp.bfloat16)
        return layer_out.reshape(req_dev, steps, width)

    return body


def solution(mesh):
    return jax.shard_map(
        make_body(mesh.shape["req"], mesh.shape["tp"]),
        mesh=mesh,
        in_specs=(
            P("req", None, None),
            P("req"),
            P("req", None),
            P("req", None, None, None),
            P(),
            P(None, "tp"),
            P(),
            P(),
            P("tp", None),
            P(),
            P(None, "tp"),
            P(None, "tp"),
            P("tp", None),
        ),
        out_specs=P("req", None, None),
        check_vma=False,
    )
```

```python
import jax
import jax.numpy as jnp
from jax import lax
from jax.sharding import PartitionSpec as P

WINDOW = 1024


negative = -1e30
epsilon = 1e-06


def rms_norm(values, gain):
    return values * lax.rsqrt(jnp.mean(values * values, axis=-1, keepdims=True) + epsilon) * gain


def staggered_sum(values, req_size, tp_size):
    steps = []
    step = 1
    while step < tp_size:
        steps.append(step)
        step *= 2
    for round_index in range(len(steps)):
        pairs = []
        for q in range(req_size):
            order = steps if q % 2 == 0 else steps[::-1]
            for t in range(tp_size):
                pairs.append((q * tp_size + t, q * tp_size + (t ^ order[round_index])))
        values = values + lax.ppermute(values, ("req", "tp"), pairs)
    return values


def make_body(req_size, tp_size):
    def body(
        tokens,
        lengths,
        page_table,
        kv_pages,
        norm_gain,
        query_weight,
        key_weight,
        value_weight,
        out_weight,
        mlp_gain,
        gate_weight,
        up_weight,
        down_weight,
    ):
        req_dev, steps, width = tokens.shape
        head_dim = key_weight.shape[1]
        heads_dev = query_weight.shape[1] // head_dim
        pool_size = kv_pages.shape[0]
        page_size = kv_pages.shape[2]
        window_pages = page_table.shape[1]
        requests = req_dev * req_size
        qwidth = steps * heads_dev * head_dim
        token_rows = tokens.reshape(req_dev * steps, width)
        normed3 = rms_norm(tokens.astype(jnp.float32), norm_gain).astype(jnp.bfloat16)
        normed = normed3.reshape(req_dev * steps, width)
        queries = (
            jnp.einsum("rsd,dh->rsh", normed3, query_weight, preferred_element_type=jnp.float32)
            * head_dim ** (-0.5)
        ).astype(jnp.bfloat16).reshape(req_dev * steps, heads_dev * head_dim)
        key_new = jnp.dot(normed, key_weight, preferred_element_type=jnp.float32).astype(jnp.bfloat16)
        value_new = jnp.dot(normed, value_weight, preferred_element_type=jnp.float32).astype(
            jnp.bfloat16
        )
        length_col = jnp.broadcast_to(lengths[:, None], (req_dev, 1))
        packed = jnp.concatenate(
            [
                queries.reshape(req_dev, qwidth),
                (page_table // 256).astype(jnp.bfloat16),
                (length_col // 256).astype(jnp.bfloat16),
                (page_table % 256).astype(jnp.bfloat16),
                (length_col % 256).astype(jnp.bfloat16),
            ],
            axis=1,
        )
        gathered = lax.all_to_all(
            jnp.broadcast_to(packed[None], (req_size,) + packed.shape), "req", 0, 0, tiled=False
        ).reshape(requests, packed.shape[1])
        all_queries = gathered[:, :qwidth].reshape(requests, steps * heads_dev, head_dim)
        nints = window_pages + 1
        digits = gathered[:, qwidth:].astype(jnp.int32)
        all_ints = digits[:, :nints] * 256 + digits[:, nints:]
        all_table = all_ints[:, :window_pages]
        all_lengths = all_ints[:, window_pages]
        flat_table = all_table.reshape(-1)
        entries = flat_table.shape[0]
        my_slots = lax.axis_index("req") * pool_size + jnp.arange(pool_size, dtype=jnp.int32)
        match = flat_table[None, :] == my_slots[:, None]
        owner_entry = jnp.sum(
            jnp.where(match, jnp.arange(entries, dtype=jnp.int32)[None, :], 0), axis=1
        )
        page_request = owner_entry // window_pages
        page_number = owner_entry % window_pages
        page_length = all_lengths[page_request]
        first_page = jnp.maximum(page_length - (WINDOW - 1), 0) // page_size
        position = (first_page + page_number)[:, None] * page_size + jnp.arange(
            page_size, dtype=jnp.int32
        )[None, :]
        current = page_length[:, None] + jnp.arange(steps, dtype=jnp.int32)[None, :]
        visible = (position[:, None, :] < page_length[:, None, None]) & (
            position[:, None, :] > current[:, :, None] - WINDOW
        )
        visible = visible[:, :, None, :]
        page_queries = all_queries[page_request]
        scores = jnp.einsum(
            "pqd,pkd->pqk", page_queries, kv_pages[:, 0], preferred_element_type=jnp.float32
        )
        scores = jnp.where(visible, scores.reshape(pool_size, steps, heads_dev, page_size), negative)
        block_max = jnp.max(scores, axis=-1)
        weights = jnp.where(visible, jnp.exp(scores - block_max[..., None]), 0.0)
        block_total = jnp.sum(weights, axis=-1)
        block_out = jnp.einsum(
            "pqk,pkd->pqd",
            weights.astype(jnp.bfloat16).reshape(pool_size, steps * heads_dev, page_size),
            kv_pages[:, 1],
            preferred_element_type=jnp.float32,
        )
        block_out = block_out.reshape(pool_size, steps, heads_dev, head_dim)
        member = page_request[None, :] == jnp.arange(requests, dtype=jnp.int32)[:, None]
        local_max = jnp.max(
            jnp.where(member[:, :, None, None], block_max[None], negative), axis=1
        )
        scale = jnp.exp(block_max - local_max[page_request])
        nsh = steps * heads_dev
        scaled = jnp.concatenate(
            [
                (block_out * scale[..., None]).reshape(pool_size, nsh * head_dim),
                (block_total * scale).reshape(pool_size, nsh),
            ],
            axis=1,
        )
        sent = jnp.dot(
            member.astype(jnp.float32),
            scaled,
            precision=lax.Precision.HIGHEST,
            preferred_element_type=jnp.float32,
        )
        flat_max = local_max.reshape(requests, nsh)
        max_hi = lax.reduce_precision(flat_max, exponent_bits=8, mantissa_bits=7)
        rest = flat_max - max_hi
        max_mid = lax.reduce_precision(rest, exponent_bits=8, mantissa_bits=7)
        max_lo = rest - max_mid
        send = jnp.concatenate(
            [sent, max_hi, max_mid, max_lo], axis=1
        ).astype(jnp.bfloat16)
        recv = lax.all_to_all(send, "req", 0, 0, tiled=True).reshape(req_size, req_dev, -1)
        got_out = (
            recv[:, :, : nsh * head_dim]
            .astype(jnp.float32)
            .reshape(req_size, req_dev, steps, heads_dev, head_dim)
        )
        got_total = (
            recv[:, :, nsh * head_dim : nsh * (head_dim + 1)]
            .astype(jnp.float32)
            .reshape(req_size, req_dev, steps, heads_dev)
        )
        pieces = recv[:, :, nsh * (head_dim + 1) :].astype(jnp.float32)
        got_max = (
            (pieces[:, :, :nsh] + pieces[:, :, nsh : 2 * nsh]) + pieces[:, :, 2 * nsh :]
        ).reshape(req_size, req_dev, steps, heads_dev)
        cache_max = jnp.max(got_max, axis=0)
        local_queries = queries.reshape(req_dev, steps, heads_dev, head_dim)
        new_scores = jnp.einsum(
            "rshd,rtd->rsht",
            local_queries,
            key_new.reshape(req_dev, steps, head_dim),
            preferred_element_type=jnp.float32,
        )
        causal = (jnp.arange(steps)[None, :] <= jnp.arange(steps)[:, None])[None, :, None, :]
        new_scores = jnp.where(causal, new_scores, negative)
        new_max = jnp.max(new_scores, axis=-1)
        new_weights = jnp.where(causal, jnp.exp(new_scores - new_max[..., None]), 0.0)
        new_total = jnp.sum(new_weights, axis=-1)
        new_out = jnp.einsum(
            "rsht,rtd->rshd",
            new_weights.astype(jnp.bfloat16),
            value_new.reshape(req_dev, steps, head_dim),
            preferred_element_type=jnp.float32,
        )
        overall = jnp.maximum(cache_max, new_max)
        src_scale = jnp.exp(got_max - overall[None])
        new_scale = jnp.exp(new_max - overall)
        total = jnp.sum(got_total * src_scale, axis=0) + new_total * new_scale
        summed = jnp.sum(got_out * src_scale[..., None], axis=0) + new_out * new_scale[..., None]
        attended = (
            (summed / total[..., None])
            .astype(jnp.bfloat16)
            .reshape(req_dev * steps, heads_dev * head_dim)
        )
        projected = jnp.dot(attended, out_weight, preferred_element_type=jnp.float32)
        attn_total = staggered_sum(projected.astype(jnp.bfloat16), req_size, tp_size).astype(jnp.float32)
        residual = (token_rows.astype(jnp.float32) + attn_total).astype(jnp.bfloat16)
        mlp_in = rms_norm(residual.astype(jnp.float32), mlp_gain).astype(jnp.bfloat16)
        gate = jnp.dot(mlp_in, gate_weight, preferred_element_type=jnp.float32)
        upward = jnp.dot(mlp_in, up_weight, preferred_element_type=jnp.float32)
        hidden = (jax.nn.gelu(gate, approximate=True) * upward).astype(jnp.bfloat16)
        mlp_part = jnp.dot(hidden, down_weight, preferred_element_type=jnp.float32).astype(
            jnp.bfloat16
        )
        mlp_total = staggered_sum(mlp_part, req_size, tp_size).astype(jnp.float32)
        layer_out = (residual.astype(jnp.float32) + mlp_total).astype(jnp.bfloat16)
        return layer_out.reshape(req_dev, steps, width)

    return body


def solution(mesh):
    return jax.shard_map(
        make_body(mesh.shape["req"], mesh.shape["tp"]),
        mesh=mesh,
        in_specs=(
            P("req", None, None),
            P("req"),
            P("req", None),
            P("req", None, None, None),
            P(),
            P(None, "tp"),
            P(),
            P(),
            P("tp", None),
            P(),
            P(None, "tp"),
            P(None, "tp"),
            P("tp", None),
        ),
        out_specs=P("req", None, None),
        check_vma=False,
    )
```

```python
import jax
import jax.numpy as jnp
from jax import lax
from jax.sharding import PartitionSpec as P

WINDOW = 1024


negative = -1e30
epsilon = 1e-06


def rms_norm(values, gain):
    return values * lax.rsqrt(jnp.mean(values * values, axis=-1, keepdims=True) + epsilon) * gain


def staggered_sum(values, req_size, tp_size):
    steps = []
    step = 1
    while step < tp_size:
        steps.append(step)
        step *= 2
    for round_index in range(len(steps)):
        pairs = []
        for q in range(req_size):
            order = steps if q % 2 == 0 else steps[::-1]
            for t in range(tp_size):
                pairs.append((q * tp_size + t, q * tp_size + (t ^ order[round_index])))
        values = values + lax.ppermute(values, ("req", "tp"), pairs)
    return values


def make_body(req_size, tp_size):
    def body(
        tokens,
        lengths,
        page_table,
        kv_pages,
        norm_gain,
        query_weight,
        key_weight,
        value_weight,
        out_weight,
        mlp_gain,
        gate_weight,
        up_weight,
        down_weight,
    ):
        req_dev, steps, width = tokens.shape
        head_dim = key_weight.shape[1]
        heads_dev = query_weight.shape[1] // head_dim
        pool_size = kv_pages.shape[0]
        page_size = kv_pages.shape[2]
        window_pages = page_table.shape[1]
        requests = req_dev * req_size
        qwidth = steps * heads_dev * head_dim
        token_rows = tokens.reshape(req_dev * steps, width)
        normed = rms_norm(token_rows.astype(jnp.float32), norm_gain).astype(jnp.bfloat16)
        queries = (
            jnp.dot(normed, query_weight, preferred_element_type=jnp.float32) * head_dim ** (-0.5)
        ).astype(jnp.bfloat16)
        key_new = jnp.dot(normed, key_weight, preferred_element_type=jnp.float32).astype(jnp.bfloat16)
        value_new = jnp.dot(normed, value_weight, preferred_element_type=jnp.float32).astype(
            jnp.bfloat16
        )
        length_col = jnp.broadcast_to(lengths[:, None], (req_dev, 1))
        packed = jnp.concatenate(
            [
                queries.reshape(req_dev, qwidth),
                (page_table // 256).astype(jnp.bfloat16),
                (length_col // 256).astype(jnp.bfloat16),
                (page_table % 256).astype(jnp.bfloat16),
                (length_col % 256).astype(jnp.bfloat16),
            ],
            axis=1,
        )
        gathered = lax.all_to_all(
            jnp.broadcast_to(packed[None], (req_size,) + packed.shape), "req", 0, 0, tiled=False
        ).reshape(requests, packed.shape[1])
        all_queries = gathered[:, :qwidth].reshape(requests, steps * heads_dev, head_dim)
        nints = window_pages + 1
        digits = gathered[:, qwidth:].astype(jnp.int32)
        all_ints = digits[:, :nints] * 256 + digits[:, nints:]
        all_table = all_ints[:, :window_pages]
        all_lengths = all_ints[:, window_pages]
        flat_table = all_table.reshape(-1)
        entries = flat_table.shape[0]
        my_slots = lax.axis_index("req") * pool_size + jnp.arange(pool_size, dtype=jnp.int32)
        match = flat_table[None, :] == my_slots[:, None]
        owner_entry = jnp.sum(
            jnp.where(match, jnp.arange(entries, dtype=jnp.int32)[None, :], 0), axis=1
        )
        page_request = owner_entry // window_pages
        page_number = owner_entry % window_pages
        entry_length = jnp.repeat(all_lengths, window_pages)
        page_length = jnp.sum(jnp.where(match, entry_length[None, :], 0), axis=1)
        first_page = jnp.maximum(page_length - (WINDOW - 1), 0) // page_size
        position = (first_page + page_number)[:, None] * page_size + jnp.arange(
            page_size, dtype=jnp.int32
        )[None, :]
        current = page_length[:, None] + jnp.arange(steps, dtype=jnp.int32)[None, :]
        visible = (position[:, None, :] < page_length[:, None, None]) & (
            position[:, None, :] > current[:, :, None] - WINDOW
        )
        visible = visible[:, :, None, :]
        page_queries = all_queries[page_request]
        scores = jnp.einsum(
            "pqd,pkd->pqk", page_queries, kv_pages[:, 0], preferred_element_type=jnp.float32
        )
        scores = jnp.where(visible, scores.reshape(pool_size, steps, heads_dev, page_size), negative)
        block_max = jnp.max(scores, axis=-1)
        weights = jnp.where(visible, jnp.exp(scores - block_max[..., None]), 0.0)
        block_total = jnp.sum(weights, axis=-1)
        block_out = jnp.einsum(
            "pqk,pkd->pqd",
            weights.astype(jnp.bfloat16).reshape(pool_size, steps * heads_dev, page_size),
            kv_pages[:, 1],
            preferred_element_type=jnp.float32,
        )
        block_out = block_out.reshape(pool_size, steps, heads_dev, head_dim)
        member = page_request[None, :] == jnp.arange(requests, dtype=jnp.int32)[:, None]
        local_max = jnp.max(
            jnp.where(member[:, :, None, None], block_max[None], negative), axis=1
        )
        same_request = page_request[:, None] == page_request[None, :]
        page_ref_max = jnp.max(
            jnp.where(same_request[:, :, None, None], block_max[None], negative), axis=1
        )
        scale = jnp.exp(block_max - page_ref_max)
        nsh = steps * heads_dev
        scaled = jnp.concatenate(
            [
                (block_out * scale[..., None]).reshape(pool_size, nsh * head_dim),
                (block_total * scale).reshape(pool_size, nsh),
            ],
            axis=1,
        )
        sent = jnp.dot(
            member.astype(jnp.float32),
            scaled,
            precision=lax.Precision.HIGHEST,
            preferred_element_type=jnp.float32,
        )
        flat_max = local_max.reshape(requests, nsh)
        max_hi = lax.reduce_precision(flat_max, exponent_bits=8, mantissa_bits=7)
        rest = flat_max - max_hi
        max_mid = lax.reduce_precision(rest, exponent_bits=8, mantissa_bits=7)
        max_lo = rest - max_mid
        send = jnp.concatenate(
            [sent, max_hi, max_mid, max_lo], axis=1
        ).astype(jnp.bfloat16)
        recv = lax.all_to_all(send, "req", 0, 0, tiled=True).reshape(req_size, req_dev, -1)
        got_out = (
            recv[:, :, : nsh * head_dim]
            .astype(jnp.float32)
            .reshape(req_size, req_dev, steps, heads_dev, head_dim)
        )
        got_total = (
            recv[:, :, nsh * head_dim : nsh * (head_dim + 1)]
            .astype(jnp.float32)
            .reshape(req_size, req_dev, steps, heads_dev)
        )
        pieces = recv[:, :, nsh * (head_dim + 1) :].astype(jnp.float32)
        got_max = (
            (pieces[:, :, :nsh] + pieces[:, :, nsh : 2 * nsh]) + pieces[:, :, 2 * nsh :]
        ).reshape(req_size, req_dev, steps, heads_dev)
        cache_max = jnp.max(got_max, axis=0)
        local_queries = queries.reshape(req_dev, steps, heads_dev, head_dim)
        new_scores = jnp.einsum(
            "rshd,rtd->rsht",
            local_queries,
            key_new.reshape(req_dev, steps, head_dim),
            preferred_element_type=jnp.float32,
        )
        causal = (jnp.arange(steps)[None, :] <= jnp.arange(steps)[:, None])[None, :, None, :]
        new_scores = jnp.where(causal, new_scores, negative)
        new_max = jnp.max(new_scores, axis=-1)
        new_weights = jnp.where(causal, jnp.exp(new_scores - new_max[..., None]), 0.0)
        new_total = jnp.sum(new_weights, axis=-1)
        new_out = jnp.einsum(
            "rsht,rtd->rshd",
            new_weights.astype(jnp.bfloat16),
            value_new.reshape(req_dev, steps, head_dim),
            preferred_element_type=jnp.float32,
        )
        overall = jnp.maximum(cache_max, new_max)
        src_scale = jnp.exp(got_max - overall[None])
        new_scale = jnp.exp(new_max - overall)
        total = jnp.sum(got_total * src_scale, axis=0) + new_total * new_scale
        summed = jnp.sum(got_out * src_scale[..., None], axis=0) + new_out * new_scale[..., None]
        attended = (
            (summed / total[..., None])
            .astype(jnp.bfloat16)
            .reshape(req_dev * steps, heads_dev * head_dim)
        )
        projected = jnp.dot(attended, out_weight, preferred_element_type=jnp.float32)
        attn_total = staggered_sum(projected.astype(jnp.bfloat16), req_size, tp_size).astype(jnp.float32)
        residual = (token_rows.astype(jnp.float32) + attn_total).astype(jnp.bfloat16)
        mlp_in = rms_norm(residual.astype(jnp.float32), mlp_gain).astype(jnp.bfloat16)
        gate = jnp.dot(mlp_in, gate_weight, preferred_element_type=jnp.float32)
        upward = jnp.dot(mlp_in, up_weight, preferred_element_type=jnp.float32)
        hidden = (jax.nn.gelu(gate, approximate=True) * upward).astype(jnp.bfloat16)
        mlp_part = jnp.dot(hidden, down_weight, preferred_element_type=jnp.float32).astype(
            jnp.bfloat16
        )
        mlp_total = staggered_sum(mlp_part, req_size, tp_size).astype(jnp.float32)
        layer_out = (residual.astype(jnp.float32) + mlp_total).astype(jnp.bfloat16)
        return layer_out.reshape(req_dev, steps, width)

    return body


def solution(mesh):
    return jax.shard_map(
        make_body(mesh.shape["req"], mesh.shape["tp"]),
        mesh=mesh,
        in_specs=(
            P("req", None, None),
            P("req"),
            P("req", None),
            P("req", None, None, None),
            P(),
            P(None, "tp"),
            P(),
            P(),
            P("tp", None),
            P(),
            P(None, "tp"),
            P(None, "tp"),
            P("tp", None),
        ),
        out_specs=P("req", None, None),
        check_vma=False,
    )
```

```python
import jax
import jax.numpy as jnp
from jax import lax
from jax.sharding import PartitionSpec as P

WINDOW = 1024


negative = -1e30
epsilon = 1e-06


def rms_norm(values, gain):
    return values * lax.rsqrt(jnp.mean(values * values, axis=-1, keepdims=True) + epsilon) * gain


def tree_sum(values, axis, size):
    step = 1
    while step < size // 2:
        values = values + lax.ppermute(values, axis, [(i, i ^ step) for i in range(size)])
        step *= 2
    if size > 1:
        values = values + lax.ppermute(values, axis, [(i, size - 1 - i) for i in range(size)])
    return values


def make_body(req_size, tp_size):
    def body(
        tokens,
        lengths,
        page_table,
        kv_pages,
        norm_gain,
        query_weight,
        key_weight,
        value_weight,
        out_weight,
        mlp_gain,
        gate_weight,
        up_weight,
        down_weight,
    ):
        req_dev, steps, width = tokens.shape
        head_dim = key_weight.shape[1]
        heads_dev = query_weight.shape[1] // head_dim
        pool_size = kv_pages.shape[0]
        page_size = kv_pages.shape[2]
        window_pages = page_table.shape[1]
        requests = req_dev * req_size
        qwidth = steps * heads_dev * head_dim
        token_rows = tokens.reshape(req_dev * steps, width)
        normed = rms_norm(token_rows.astype(jnp.float32), norm_gain).astype(jnp.bfloat16)
        queries = (
            jnp.dot(normed, query_weight, preferred_element_type=jnp.float32) * head_dim ** (-0.5)
        ).astype(jnp.bfloat16)
        key_new = jnp.dot(normed, key_weight, preferred_element_type=jnp.float32).astype(jnp.bfloat16)
        value_new = jnp.dot(normed, value_weight, preferred_element_type=jnp.float32).astype(
            jnp.bfloat16
        )
        length_col = jnp.broadcast_to(lengths[:, None], (req_dev, 1))
        packed = jnp.concatenate(
            [
                queries.reshape(req_dev, qwidth),
                (page_table // 256).astype(jnp.bfloat16),
                (length_col // 256).astype(jnp.bfloat16),
                (page_table % 256).astype(jnp.bfloat16),
                (length_col % 256).astype(jnp.bfloat16),
            ],
            axis=1,
        )
        gathered = lax.all_to_all(
            jnp.broadcast_to(packed[None], (req_size,) + packed.shape), "req", 0, 0, tiled=False
        ).reshape(requests, packed.shape[1])
        all_queries = gathered[:, :qwidth].reshape(requests, steps * heads_dev, head_dim)
        nints = window_pages + 1
        digits = gathered[:, qwidth:].astype(jnp.int32)
        all_ints = digits[:, :nints] * 256 + digits[:, nints:]
        all_table = all_ints[:, :window_pages]
        all_lengths = all_ints[:, window_pages]
        flat_table = all_table.reshape(-1)
        entries = flat_table.shape[0]
        my_slots = lax.axis_index("req") * pool_size + jnp.arange(pool_size, dtype=jnp.int32)
        match = flat_table[None, :] == my_slots[:, None]
        owner_entry = jnp.sum(
            jnp.where(match, jnp.arange(entries, dtype=jnp.int32)[None, :], 0), axis=1
        )
        page_request = owner_entry // window_pages
        page_number = owner_entry % window_pages
        entry_length = jnp.repeat(all_lengths, window_pages)
        page_length = jnp.sum(jnp.where(match, entry_length[None, :], 0), axis=1)
        first_page = jnp.maximum(page_length - (WINDOW - 1), 0) // page_size
        position = (first_page + page_number)[:, None] * page_size + jnp.arange(
            page_size, dtype=jnp.int32
        )[None, :]
        current = page_length[:, None] + jnp.arange(steps, dtype=jnp.int32)[None, :]
        visible = (position[:, None, :] < page_length[:, None, None]) & (
            position[:, None, :] > current[:, :, None] - WINDOW
        )
        visible = visible[:, :, None, :]
        page_queries = all_queries[page_request]
        scores = jnp.einsum(
            "pqd,pkd->pqk", page_queries, kv_pages[:, 0], preferred_element_type=jnp.float32
        )
        scores = jnp.where(visible, scores.reshape(pool_size, steps, heads_dev, page_size), negative)
        block_max = jnp.max(scores, axis=-1)
        weights = jnp.where(visible, jnp.exp(scores - block_max[..., None]), 0.0)
        block_total = jnp.sum(weights, axis=-1)
        block_out = jnp.einsum(
            "pqk,pkd->pqd",
            weights.astype(jnp.bfloat16).reshape(pool_size, steps * heads_dev, page_size),
            kv_pages[:, 1],
            preferred_element_type=jnp.float32,
        )
        block_out = block_out.reshape(pool_size, steps, heads_dev, head_dim)
        member = page_request[None, :] == jnp.arange(requests, dtype=jnp.int32)[:, None]
        local_max = jnp.max(
            jnp.where(member[:, :, None, None], block_max[None], negative), axis=1
        )
        same_request = page_request[:, None] == page_request[None, :]
        page_ref_max = jnp.max(
            jnp.where(same_request[:, :, None, None], block_max[None], negative), axis=1
        )
        scale = jnp.exp(block_max - page_ref_max)
        nsh = steps * heads_dev
        scaled = jnp.concatenate(
            [
                (block_out * scale[..., None]).reshape(pool_size, nsh * head_dim),
                (block_total * scale).reshape(pool_size, nsh),
            ],
            axis=1,
        )
        sent = jnp.dot(
            member.astype(jnp.float32),
            scaled,
            precision=lax.Precision.HIGHEST,
            preferred_element_type=jnp.float32,
        )
        flat_max = local_max.reshape(requests, nsh)
        max_hi = lax.reduce_precision(flat_max, exponent_bits=8, mantissa_bits=7)
        rest = flat_max - max_hi
        max_mid = lax.reduce_precision(rest, exponent_bits=8, mantissa_bits=7)
        max_lo = rest - max_mid
        send = jnp.concatenate(
            [sent, max_hi, max_mid, max_lo], axis=1
        ).astype(jnp.bfloat16)
        recv = lax.all_to_all(send, "req", 0, 0, tiled=True).reshape(req_size, req_dev, -1)
        got_out = (
            recv[:, :, : nsh * head_dim]
            .astype(jnp.float32)
            .reshape(req_size, req_dev, steps, heads_dev, head_dim)
        )
        got_total = (
            recv[:, :, nsh * head_dim : nsh * (head_dim + 1)]
            .astype(jnp.float32)
            .reshape(req_size, req_dev, steps, heads_dev)
        )
        pieces = recv[:, :, nsh * (head_dim + 1) :].astype(jnp.float32)
        got_max = (
            (pieces[:, :, :nsh] + pieces[:, :, nsh : 2 * nsh]) + pieces[:, :, 2 * nsh :]
        ).reshape(req_size, req_dev, steps, heads_dev)
        cache_max = jnp.max(got_max, axis=0)
        local_queries = queries.reshape(req_dev, steps, heads_dev, head_dim)
        new_scores = jnp.einsum(
            "rshd,rtd->rsht",
            local_queries,
            key_new.reshape(req_dev, steps, head_dim),
            preferred_element_type=jnp.float32,
        )
        causal = (jnp.arange(steps)[None, :] <= jnp.arange(steps)[:, None])[None, :, None, :]
        new_scores = jnp.where(causal, new_scores, negative)
        new_max = jnp.max(new_scores, axis=-1)
        new_weights = jnp.where(causal, jnp.exp(new_scores - new_max[..., None]), 0.0)
        new_total = jnp.sum(new_weights, axis=-1)
        new_out = jnp.einsum(
            "rsht,rtd->rshd",
            new_weights.astype(jnp.bfloat16),
            value_new.reshape(req_dev, steps, head_dim),
            preferred_element_type=jnp.float32,
        )
        overall = jnp.maximum(cache_max, new_max)
        src_scale = jnp.exp(got_max - overall[None])
        new_scale = jnp.exp(new_max - overall)
        total = jnp.sum(got_total * src_scale, axis=0) + new_total * new_scale
        summed = jnp.sum(got_out * src_scale[..., None], axis=0) + new_out * new_scale[..., None]
        attended = (
            (summed / total[..., None])
            .astype(jnp.bfloat16)
            .reshape(req_dev * steps, heads_dev * head_dim)
        )
        projected = jnp.dot(attended, out_weight, preferred_element_type=jnp.float32)
        attn_total = tree_sum(projected.astype(jnp.bfloat16), "tp", tp_size).astype(jnp.float32)
        residual = (token_rows.astype(jnp.float32) + attn_total).astype(jnp.bfloat16)
        mlp_in = rms_norm(residual.astype(jnp.float32), mlp_gain).astype(jnp.bfloat16)
        gate = jnp.dot(mlp_in, gate_weight, preferred_element_type=jnp.float32)
        upward = jnp.dot(mlp_in, up_weight, preferred_element_type=jnp.float32)
        hidden = (jax.nn.gelu(gate, approximate=True) * upward).astype(jnp.bfloat16)
        mlp_part = jnp.dot(hidden, down_weight, preferred_element_type=jnp.float32).astype(
            jnp.bfloat16
        )
        mlp_total = tree_sum(mlp_part, "tp", tp_size).astype(jnp.float32)
        layer_out = (residual.astype(jnp.float32) + mlp_total).astype(jnp.bfloat16)
        return layer_out.reshape(req_dev, steps, width)

    return body


def solution(mesh):
    return jax.shard_map(
        make_body(mesh.shape["req"], mesh.shape["tp"]),
        mesh=mesh,
        in_specs=(
            P("req", None, None),
            P("req"),
            P("req", None),
            P("req", None, None, None),
            P(),
            P(None, "tp"),
            P(),
            P(),
            P("tp", None),
            P(),
            P(None, "tp"),
            P(None, "tp"),
            P("tp", None),
        ),
        out_specs=P("req", None, None),
        check_vma=False,
    )
```

```python
import jax
import jax.numpy as jnp
from jax import lax
from jax.sharding import PartitionSpec as P

WINDOW = 1024


negative = -1e30
epsilon = 1e-06


def rms_norm(values, gain):
    return values * lax.rsqrt(jnp.mean(values * values, axis=-1, keepdims=True) + epsilon) * gain


def tree_sum(values, axis, size, first_step=1):
    step = first_step
    while step < size // 2:
        values = values + lax.ppermute(values, axis, [(i, i ^ step) for i in range(size)])
        step *= 2
    if size > 1:
        values = values + lax.ppermute(values, axis, [(i, size - 1 - i) for i in range(size)])
    return values


def make_body(req_size, tp_size):
    def body(
        tokens,
        lengths,
        page_table,
        kv_pages,
        norm_gain,
        query_weight,
        key_weight,
        value_weight,
        out_weight,
        mlp_gain,
        gate_weight,
        up_weight,
        down_weight,
    ):
        req_dev, steps, width = tokens.shape
        head_dim = key_weight.shape[1]
        heads_dev = query_weight.shape[1] // head_dim
        pool_size = kv_pages.shape[0]
        page_size = kv_pages.shape[2]
        window_pages = page_table.shape[1]
        requests = req_dev * req_size
        qwidth = steps * heads_dev * head_dim
        token_rows = tokens.reshape(req_dev * steps, width)
        partner_weight = lax.ppermute(out_weight, "tp", [(i, i ^ 1) for i in range(tp_size)])
        normed = rms_norm(token_rows.astype(jnp.float32), norm_gain).astype(jnp.bfloat16)
        queries = (
            jnp.dot(normed, query_weight, preferred_element_type=jnp.float32) * head_dim ** (-0.5)
        ).astype(jnp.bfloat16)
        key_new = jnp.dot(normed, key_weight, preferred_element_type=jnp.float32).astype(jnp.bfloat16)
        value_new = jnp.dot(normed, value_weight, preferred_element_type=jnp.float32).astype(
            jnp.bfloat16
        )
        length_col = jnp.broadcast_to(lengths[:, None], (req_dev, 1))
        packed = jnp.concatenate(
            [
                queries.reshape(req_dev, qwidth),
                (page_table // 256).astype(jnp.bfloat16),
                (length_col // 256).astype(jnp.bfloat16),
                (page_table % 256).astype(jnp.bfloat16),
                (length_col % 256).astype(jnp.bfloat16),
            ],
            axis=1,
        )
        gathered = lax.all_to_all(
            jnp.broadcast_to(packed[None], (req_size,) + packed.shape), "req", 0, 0, tiled=False
        ).reshape(requests, packed.shape[1])
        all_queries = gathered[:, :qwidth].reshape(requests, steps * heads_dev, head_dim)
        nints = window_pages + 1
        digits = gathered[:, qwidth:].astype(jnp.int32)
        all_ints = digits[:, :nints] * 256 + digits[:, nints:]
        all_table = all_ints[:, :window_pages]
        all_lengths = all_ints[:, window_pages]
        flat_table = all_table.reshape(-1)
        entries = flat_table.shape[0]
        my_slots = lax.axis_index("req") * pool_size + jnp.arange(pool_size, dtype=jnp.int32)
        match = flat_table[None, :] == my_slots[:, None]
        owner_entry = jnp.sum(
            jnp.where(match, jnp.arange(entries, dtype=jnp.int32)[None, :], 0), axis=1
        )
        page_request = owner_entry // window_pages
        page_number = owner_entry % window_pages
        entry_length = jnp.repeat(all_lengths, window_pages)
        page_length = jnp.sum(jnp.where(match, entry_length[None, :], 0), axis=1)
        first_page = jnp.maximum(page_length - (WINDOW - 1), 0) // page_size
        position = (first_page + page_number)[:, None] * page_size + jnp.arange(
            page_size, dtype=jnp.int32
        )[None, :]
        current = page_length[:, None] + jnp.arange(steps, dtype=jnp.int32)[None, :]
        visible = (position[:, None, :] < page_length[:, None, None]) & (
            position[:, None, :] > current[:, :, None] - WINDOW
        )
        visible = visible[:, :, None, :]
        page_queries = all_queries[page_request]
        scores = jnp.einsum(
            "pqd,pkd->pqk", page_queries, kv_pages[:, 0], preferred_element_type=jnp.float32
        )
        scores = jnp.where(visible, scores.reshape(pool_size, steps, heads_dev, page_size), negative)
        block_max = jnp.max(scores, axis=-1)
        weights = jnp.where(visible, jnp.exp(scores - block_max[..., None]), 0.0)
        block_total = jnp.sum(weights, axis=-1)
        block_out = jnp.einsum(
            "pqk,pkd->pqd",
            weights.astype(jnp.bfloat16).reshape(pool_size, steps * heads_dev, page_size),
            kv_pages[:, 1],
            preferred_element_type=jnp.float32,
        )
        block_out = block_out.reshape(pool_size, steps, heads_dev, head_dim)
        member = page_request[None, :] == jnp.arange(requests, dtype=jnp.int32)[:, None]
        local_max = jnp.max(
            jnp.where(member[:, :, None, None], block_max[None], negative), axis=1
        )
        same_request = page_request[:, None] == page_request[None, :]
        page_ref_max = jnp.max(
            jnp.where(same_request[:, :, None, None], block_max[None], negative), axis=1
        )
        scale = jnp.exp(block_max - page_ref_max)
        nsh = steps * heads_dev
        scaled = jnp.concatenate(
            [
                (block_out * scale[..., None]).reshape(pool_size, nsh * head_dim),
                (block_total * scale).reshape(pool_size, nsh),
            ],
            axis=1,
        )
        sent = jnp.dot(
            member.astype(jnp.float32),
            scaled,
            precision=lax.Precision.HIGHEST,
            preferred_element_type=jnp.float32,
        )
        flat_max = local_max.reshape(requests, nsh)
        max_hi = lax.reduce_precision(flat_max, exponent_bits=8, mantissa_bits=7)
        rest = flat_max - max_hi
        max_mid = lax.reduce_precision(rest, exponent_bits=8, mantissa_bits=7)
        max_lo = rest - max_mid
        send = jnp.concatenate(
            [sent, max_hi, max_mid, max_lo], axis=1
        ).astype(jnp.bfloat16)
        recv = lax.all_to_all(send, "req", 0, 0, tiled=True).reshape(req_size, req_dev, -1)
        got_out = (
            recv[:, :, : nsh * head_dim]
            .astype(jnp.float32)
            .reshape(req_size, req_dev, steps, heads_dev, head_dim)
        )
        got_total = (
            recv[:, :, nsh * head_dim : nsh * (head_dim + 1)]
            .astype(jnp.float32)
            .reshape(req_size, req_dev, steps, heads_dev)
        )
        pieces = recv[:, :, nsh * (head_dim + 1) :].astype(jnp.float32)
        got_max = (
            (pieces[:, :, :nsh] + pieces[:, :, nsh : 2 * nsh]) + pieces[:, :, 2 * nsh :]
        ).reshape(req_size, req_dev, steps, heads_dev)
        cache_max = jnp.max(got_max, axis=0)
        local_queries = queries.reshape(req_dev, steps, heads_dev, head_dim)
        new_scores = jnp.einsum(
            "rshd,rtd->rsht",
            local_queries,
            key_new.reshape(req_dev, steps, head_dim),
            preferred_element_type=jnp.float32,
        )
        causal = (jnp.arange(steps)[None, :] <= jnp.arange(steps)[:, None])[None, :, None, :]
        new_scores = jnp.where(causal, new_scores, negative)
        new_max = jnp.max(new_scores, axis=-1)
        new_weights = jnp.where(causal, jnp.exp(new_scores - new_max[..., None]), 0.0)
        new_total = jnp.sum(new_weights, axis=-1)
        new_out = jnp.einsum(
            "rsht,rtd->rshd",
            new_weights.astype(jnp.bfloat16),
            value_new.reshape(req_dev, steps, head_dim),
            preferred_element_type=jnp.float32,
        )
        overall = jnp.maximum(cache_max, new_max)
        src_scale = jnp.exp(got_max - overall[None])
        new_scale = jnp.exp(new_max - overall)
        total = jnp.sum(got_total * src_scale, axis=0) + new_total * new_scale
        summed = jnp.sum(got_out * src_scale[..., None], axis=0) + new_out * new_scale[..., None]
        attended = (
            (summed / total[..., None])
            .astype(jnp.bfloat16)
            .reshape(req_dev * steps, heads_dev * head_dim)
        )
        pair = [(i, i ^ 1) for i in range(tp_size)]
        other_head = lax.ppermute(attended, "tp", pair)
        lower = lax.axis_index("tp") % 2 == 0
        pair_heads = jnp.concatenate(
            [jnp.where(lower, attended, other_head), jnp.where(lower, other_head, attended)], axis=1
        )
        pair_weight = jnp.concatenate(
            [jnp.where(lower, out_weight, partner_weight), jnp.where(lower, partner_weight, out_weight)],
            axis=0,
        )
        projected = jnp.dot(pair_heads, pair_weight, preferred_element_type=jnp.float32)
        attn_total = tree_sum(
            projected.astype(jnp.bfloat16), "tp", tp_size, first_step=2
        ).astype(jnp.float32)
        residual = (token_rows.astype(jnp.float32) + attn_total).astype(jnp.bfloat16)
        mlp_in = rms_norm(residual.astype(jnp.float32), mlp_gain).astype(jnp.bfloat16)
        gate = jnp.dot(mlp_in, gate_weight, preferred_element_type=jnp.float32)
        upward = jnp.dot(mlp_in, up_weight, preferred_element_type=jnp.float32)
        hidden = (jax.nn.gelu(gate, approximate=True) * upward).astype(jnp.bfloat16)
        mlp_part = jnp.dot(hidden, down_weight, preferred_element_type=jnp.float32).astype(
            jnp.bfloat16
        )
        mlp_total = tree_sum(mlp_part, "tp", tp_size).astype(jnp.float32)
        layer_out = (residual.astype(jnp.float32) + mlp_total).astype(jnp.bfloat16)
        return layer_out.reshape(req_dev, steps, width)

    return body


def solution(mesh):
    return jax.shard_map(
        make_body(mesh.shape["req"], mesh.shape["tp"]),
        mesh=mesh,
        in_specs=(
            P("req", None, None),
            P("req"),
            P("req", None),
            P("req", None, None, None),
            P(),
            P(None, "tp"),
            P(),
            P(),
            P("tp", None),
            P(),
            P(None, "tp"),
            P(None, "tp"),
            P("tp", None),
        ),
        out_specs=P("req", None, None),
        check_vma=False,
    )
```

```python
import jax
import jax.numpy as jnp
from jax import lax
from jax.sharding import PartitionSpec as P

WINDOW = 1024


negative = -1e30
epsilon = 1e-06


def rms_norm(values, gain):
    return values * lax.rsqrt(jnp.mean(values * values, axis=-1, keepdims=True) + epsilon) * gain


def tree_sum(values, axis, size, first_step=1):
    step = first_step
    while step < size // 2:
        values = values + lax.ppermute(values, axis, [(i, i ^ step) for i in range(size)])
        step *= 2
    if size > 1:
        values = values + lax.ppermute(values, axis, [(i, size - 1 - i) for i in range(size)])
    return values


def make_body(req_size, tp_size):
    def body(
        tokens,
        lengths,
        page_table,
        kv_pages,
        norm_gain,
        query_weight,
        key_weight,
        value_weight,
        out_weight,
        mlp_gain,
        gate_weight,
        up_weight,
        down_weight,
    ):
        req_dev, steps, width = tokens.shape
        head_dim = key_weight.shape[1]
        heads_dev = query_weight.shape[1] // head_dim
        pool_size = kv_pages.shape[0]
        page_size = kv_pages.shape[2]
        window_pages = page_table.shape[1]
        requests = req_dev * req_size
        qwidth = steps * heads_dev * head_dim
        token_rows = tokens.reshape(req_dev * steps, width)
        partner_weight = lax.ppermute(out_weight, "tp", [(i, i ^ 1) for i in range(tp_size)])
        normed = rms_norm(token_rows.astype(jnp.float32), norm_gain).astype(jnp.bfloat16)
        queries = (
            jnp.dot(normed, query_weight, preferred_element_type=jnp.float32) * head_dim ** (-0.5)
        ).astype(jnp.bfloat16)
        key_new = jnp.dot(normed, key_weight, preferred_element_type=jnp.float32).astype(jnp.bfloat16)
        value_new = jnp.dot(normed, value_weight, preferred_element_type=jnp.float32).astype(
            jnp.bfloat16
        )
        length_col = jnp.broadcast_to(lengths[:, None], (req_dev, 1))
        packed = jnp.concatenate(
            [
                queries.reshape(req_dev, qwidth),
                (page_table // 256).astype(jnp.bfloat16),
                (length_col // 256).astype(jnp.bfloat16),
                (page_table % 256).astype(jnp.bfloat16),
                (length_col % 256).astype(jnp.bfloat16),
            ],
            axis=1,
        )
        gathered = lax.all_to_all(
            jnp.broadcast_to(packed[None], (req_size,) + packed.shape), "req", 0, 0, tiled=False
        ).reshape(requests, packed.shape[1])
        all_queries = gathered[:, :qwidth].reshape(requests, steps * heads_dev, head_dim)
        nints = window_pages + 1
        digits = gathered[:, qwidth:].astype(jnp.int32)
        all_ints = digits[:, :nints] * 256 + digits[:, nints:]
        all_table = all_ints[:, :window_pages]
        all_lengths = all_ints[:, window_pages]
        flat_table = all_table.reshape(-1)
        entries = flat_table.shape[0]
        my_slots = lax.axis_index("req") * pool_size + jnp.arange(pool_size, dtype=jnp.int32)
        match = flat_table[None, :] == my_slots[:, None]
        owner_entry = jnp.sum(
            jnp.where(match, jnp.arange(entries, dtype=jnp.int32)[None, :], 0), axis=1
        )
        page_request = owner_entry // window_pages
        page_number = owner_entry % window_pages
        entry_length = jnp.repeat(all_lengths, window_pages)
        page_length = jnp.sum(jnp.where(match, entry_length[None, :], 0), axis=1)
        first_page = jnp.maximum(page_length - (WINDOW - 1), 0) // page_size
        position = (first_page + page_number)[:, None] * page_size + jnp.arange(
            page_size, dtype=jnp.int32
        )[None, :]
        current = page_length[:, None] + jnp.arange(steps, dtype=jnp.int32)[None, :]
        visible = (position[:, None, :] < page_length[:, None, None]) & (
            position[:, None, :] > current[:, :, None] - WINDOW
        )
        visible = visible[:, :, None, :]
        page_queries = all_queries[page_request]
        scores = jnp.einsum(
            "pqd,pkd->pqk", page_queries, kv_pages[:, 0], preferred_element_type=jnp.float32
        )
        scores = jnp.where(visible, scores.reshape(pool_size, steps, heads_dev, page_size), negative)
        block_max = jnp.max(scores, axis=-1)
        weights = jnp.where(visible, jnp.exp(scores - block_max[..., None]), 0.0)
        block_total = jnp.sum(weights, axis=-1)
        block_out = jnp.einsum(
            "pqk,pkd->pqd",
            weights.astype(jnp.bfloat16).reshape(pool_size, steps * heads_dev, page_size),
            kv_pages[:, 1],
            preferred_element_type=jnp.float32,
        )
        block_out = block_out.reshape(pool_size, steps, heads_dev, head_dim)
        member = page_request[None, :] == jnp.arange(requests, dtype=jnp.int32)[:, None]
        local_max = jnp.max(
            jnp.where(member[:, :, None, None], block_max[None], negative), axis=1
        )
        same_request = page_request[:, None] == page_request[None, :]
        page_ref_max = jnp.max(
            jnp.where(same_request[:, :, None, None], block_max[None], negative), axis=1
        )
        scale = jnp.exp(block_max - page_ref_max)
        nsh = steps * heads_dev
        scaled = jnp.concatenate(
            [
                (block_out * scale[..., None]).reshape(pool_size, nsh * head_dim),
                (block_total * scale).reshape(pool_size, nsh),
            ],
            axis=1,
        )
        sent = jnp.dot(
            member.astype(jnp.float32),
            scaled,
            precision=lax.Precision.HIGHEST,
            preferred_element_type=jnp.float32,
        )
        flat_max = local_max.reshape(requests, nsh)
        max_hi = lax.reduce_precision(flat_max, exponent_bits=8, mantissa_bits=7)
        rest = flat_max - max_hi
        max_mid = lax.reduce_precision(rest, exponent_bits=8, mantissa_bits=7)
        max_lo = rest - max_mid
        send = jnp.concatenate(
            [sent, max_hi, max_mid, max_lo], axis=1
        ).astype(jnp.bfloat16)
        recv = lax.all_to_all(send, "req", 0, 0, tiled=True).reshape(req_size, req_dev, -1)
        got_out = (
            recv[:, :, : nsh * head_dim]
            .astype(jnp.float32)
            .reshape(req_size, req_dev, steps, heads_dev, head_dim)
        )
        got_total = (
            recv[:, :, nsh * head_dim : nsh * (head_dim + 1)]
            .astype(jnp.float32)
            .reshape(req_size, req_dev, steps, heads_dev)
        )
        pieces = recv[:, :, nsh * (head_dim + 1) :].astype(jnp.float32)
        got_max = (
            (pieces[:, :, :nsh] + pieces[:, :, nsh : 2 * nsh]) + pieces[:, :, 2 * nsh :]
        ).reshape(req_size, req_dev, steps, heads_dev)
        cache_max = jnp.max(got_max, axis=0)
        local_queries = queries.reshape(req_dev, steps, heads_dev, head_dim)
        new_scores = jnp.einsum(
            "rshd,rtd->rsht",
            local_queries,
            key_new.reshape(req_dev, steps, head_dim),
            preferred_element_type=jnp.float32,
        )
        causal = (jnp.arange(steps)[None, :] <= jnp.arange(steps)[:, None])[None, :, None, :]
        new_scores = jnp.where(causal, new_scores, negative)
        new_max = jnp.max(new_scores, axis=-1)
        new_weights = jnp.where(causal, jnp.exp(new_scores - new_max[..., None]), 0.0)
        new_total = jnp.sum(new_weights, axis=-1)
        new_out = jnp.einsum(
            "rsht,rtd->rshd",
            new_weights.astype(jnp.bfloat16),
            value_new.reshape(req_dev, steps, head_dim),
            preferred_element_type=jnp.float32,
        )
        overall = jnp.maximum(cache_max, new_max)
        src_scale = jnp.exp(got_max - overall[None])
        new_scale = jnp.exp(new_max - overall)
        total = jnp.sum(got_total * src_scale, axis=0) + new_total * new_scale
        summed = jnp.sum(got_out * src_scale[..., None], axis=0) + new_out * new_scale[..., None]
        attended = (
            (summed / total[..., None])
            .astype(jnp.bfloat16)
            .reshape(req_dev * steps, heads_dev * head_dim)
        )
        pair = [(i, i ^ 1) for i in range(tp_size)]
        other_head = lax.ppermute(attended, "tp", pair)
        projected = jnp.dot(attended, out_weight, preferred_element_type=jnp.float32) + jnp.dot(
            other_head, partner_weight, preferred_element_type=jnp.float32
        )
        attn_total = tree_sum(
            projected.astype(jnp.bfloat16), "tp", tp_size, first_step=2
        ).astype(jnp.float32)
        residual = (token_rows.astype(jnp.float32) + attn_total).astype(jnp.bfloat16)
        mlp_in = rms_norm(residual.astype(jnp.float32), mlp_gain).astype(jnp.bfloat16)
        gate = jnp.dot(mlp_in, gate_weight, preferred_element_type=jnp.float32)
        upward = jnp.dot(mlp_in, up_weight, preferred_element_type=jnp.float32)
        hidden = (jax.nn.gelu(gate, approximate=True) * upward).astype(jnp.bfloat16)
        mlp_part = jnp.dot(hidden, down_weight, preferred_element_type=jnp.float32).astype(
            jnp.bfloat16
        )
        mlp_total = tree_sum(mlp_part, "tp", tp_size).astype(jnp.float32)
        layer_out = (residual.astype(jnp.float32) + mlp_total).astype(jnp.bfloat16)
        return layer_out.reshape(req_dev, steps, width)

    return body


def solution(mesh):
    return jax.shard_map(
        make_body(mesh.shape["req"], mesh.shape["tp"]),
        mesh=mesh,
        in_specs=(
            P("req", None, None),
            P("req"),
            P("req", None),
            P("req", None, None, None),
            P(),
            P(None, "tp"),
            P(),
            P(),
            P("tp", None),
            P(),
            P(None, "tp"),
            P(None, "tp"),
            P("tp", None),
        ),
        out_specs=P("req", None, None),
        check_vma=False,
    )
```

```python
import jax
import jax.numpy as jnp
from jax import lax
from jax.sharding import PartitionSpec as P

WINDOW = 1024


negative = -1e30
epsilon = 1e-06


def rms_norm(values, gain):
    return values * lax.rsqrt(jnp.mean(values * values, axis=-1, keepdims=True) + epsilon) * gain


def tree_sum(values, axis, size, first_step=1):
    step = first_step
    while step < size // 2:
        values = values + lax.ppermute(values, axis, [(i, i ^ step) for i in range(size)])
        step *= 2
    if size > 1:
        values = values + lax.ppermute(values, axis, [(i, size - 1 - i) for i in range(size)])
    return values


def make_body(req_size, tp_size):
    def body(
        tokens,
        lengths,
        page_table,
        kv_pages,
        norm_gain,
        query_weight,
        key_weight,
        value_weight,
        out_weight,
        mlp_gain,
        gate_weight,
        up_weight,
        down_weight,
    ):
        req_dev, steps, width = tokens.shape
        head_dim = key_weight.shape[1]
        heads_dev = query_weight.shape[1] // head_dim
        pool_size = kv_pages.shape[0]
        page_size = kv_pages.shape[2]
        window_pages = page_table.shape[1]
        requests = req_dev * req_size
        qwidth = steps * heads_dev * head_dim
        token_rows = tokens.reshape(req_dev * steps, width)
        partner_weight = lax.ppermute(out_weight, "tp", [(i, i ^ 1) for i in range(tp_size)])
        lower = lax.axis_index("tp") % 2 == 0
        pair_weight = jnp.concatenate(
            [jnp.where(lower, out_weight, partner_weight), jnp.where(lower, partner_weight, out_weight)],
            axis=0,
        )
        far_weight = lax.ppermute(pair_weight, "tp", [(i, i ^ 2) for i in range(tp_size)])
        normed = rms_norm(token_rows.astype(jnp.float32), norm_gain).astype(jnp.bfloat16)
        queries = (
            jnp.dot(normed, query_weight, preferred_element_type=jnp.float32) * head_dim ** (-0.5)
        ).astype(jnp.bfloat16)
        key_new = jnp.dot(normed, key_weight, preferred_element_type=jnp.float32).astype(jnp.bfloat16)
        value_new = jnp.dot(normed, value_weight, preferred_element_type=jnp.float32).astype(
            jnp.bfloat16
        )
        length_col = jnp.broadcast_to(lengths[:, None], (req_dev, 1))
        packed = jnp.concatenate(
            [
                queries.reshape(req_dev, qwidth),
                (page_table // 256).astype(jnp.bfloat16),
                (length_col // 256).astype(jnp.bfloat16),
                (page_table % 256).astype(jnp.bfloat16),
                (length_col % 256).astype(jnp.bfloat16),
            ],
            axis=1,
        )
        gathered = lax.all_to_all(
            jnp.broadcast_to(packed[None], (req_size,) + packed.shape), "req", 0, 0, tiled=False
        ).reshape(requests, packed.shape[1])
        all_queries = gathered[:, :qwidth].reshape(requests, steps * heads_dev, head_dim)
        nints = window_pages + 1
        digits = gathered[:, qwidth:].astype(jnp.int32)
        all_ints = digits[:, :nints] * 256 + digits[:, nints:]
        all_table = all_ints[:, :window_pages]
        all_lengths = all_ints[:, window_pages]
        flat_table = all_table.reshape(-1)
        entries = flat_table.shape[0]
        my_slots = lax.axis_index("req") * pool_size + jnp.arange(pool_size, dtype=jnp.int32)
        match = flat_table[None, :] == my_slots[:, None]
        owner_entry = jnp.sum(
            jnp.where(match, jnp.arange(entries, dtype=jnp.int32)[None, :], 0), axis=1
        )
        page_request = owner_entry // window_pages
        page_number = owner_entry % window_pages
        entry_length = jnp.repeat(all_lengths, window_pages)
        page_length = jnp.sum(jnp.where(match, entry_length[None, :], 0), axis=1)
        first_page = jnp.maximum(page_length - (WINDOW - 1), 0) // page_size
        position = (first_page + page_number)[:, None] * page_size + jnp.arange(
            page_size, dtype=jnp.int32
        )[None, :]
        current = page_length[:, None] + jnp.arange(steps, dtype=jnp.int32)[None, :]
        visible = (position[:, None, :] < page_length[:, None, None]) & (
            position[:, None, :] > current[:, :, None] - WINDOW
        )
        visible = visible[:, :, None, :]
        page_queries = all_queries[page_request]
        scores = jnp.einsum(
            "pqd,pkd->pqk", page_queries, kv_pages[:, 0], preferred_element_type=jnp.float32
        )
        scores = jnp.where(visible, scores.reshape(pool_size, steps, heads_dev, page_size), negative)
        block_max = jnp.max(scores, axis=-1)
        weights = jnp.where(visible, jnp.exp(scores - block_max[..., None]), 0.0)
        block_total = jnp.sum(weights, axis=-1)
        block_out = jnp.einsum(
            "pqk,pkd->pqd",
            weights.astype(jnp.bfloat16).reshape(pool_size, steps * heads_dev, page_size),
            kv_pages[:, 1],
            preferred_element_type=jnp.float32,
        )
        block_out = block_out.reshape(pool_size, steps, heads_dev, head_dim)
        member = page_request[None, :] == jnp.arange(requests, dtype=jnp.int32)[:, None]
        local_max = jnp.max(
            jnp.where(member[:, :, None, None], block_max[None], negative), axis=1
        )
        same_request = page_request[:, None] == page_request[None, :]
        page_ref_max = jnp.max(
            jnp.where(same_request[:, :, None, None], block_max[None], negative), axis=1
        )
        scale = jnp.exp(block_max - page_ref_max)
        nsh = steps * heads_dev
        scaled = jnp.concatenate(
            [
                (block_out * scale[..., None]).reshape(pool_size, nsh * head_dim),
                (block_total * scale).reshape(pool_size, nsh),
            ],
            axis=1,
        )
        sent = jnp.dot(
            member.astype(jnp.float32),
            scaled,
            precision=lax.Precision.HIGHEST,
            preferred_element_type=jnp.float32,
        )
        flat_max = local_max.reshape(requests, nsh)
        max_hi = lax.reduce_precision(flat_max, exponent_bits=8, mantissa_bits=7)
        rest = flat_max - max_hi
        max_mid = lax.reduce_precision(rest, exponent_bits=8, mantissa_bits=7)
        max_lo = rest - max_mid
        send = jnp.concatenate(
            [sent, max_hi, max_mid, max_lo], axis=1
        ).astype(jnp.bfloat16)
        recv = lax.all_to_all(send, "req", 0, 0, tiled=True).reshape(req_size, req_dev, -1)
        got_out = (
            recv[:, :, : nsh * head_dim]
            .astype(jnp.float32)
            .reshape(req_size, req_dev, steps, heads_dev, head_dim)
        )
        got_total = (
            recv[:, :, nsh * head_dim : nsh * (head_dim + 1)]
            .astype(jnp.float32)
            .reshape(req_size, req_dev, steps, heads_dev)
        )
        pieces = recv[:, :, nsh * (head_dim + 1) :].astype(jnp.float32)
        got_max = (
            (pieces[:, :, :nsh] + pieces[:, :, nsh : 2 * nsh]) + pieces[:, :, 2 * nsh :]
        ).reshape(req_size, req_dev, steps, heads_dev)
        cache_max = jnp.max(got_max, axis=0)
        local_queries = queries.reshape(req_dev, steps, heads_dev, head_dim)
        new_scores = jnp.einsum(
            "rshd,rtd->rsht",
            local_queries,
            key_new.reshape(req_dev, steps, head_dim),
            preferred_element_type=jnp.float32,
        )
        causal = (jnp.arange(steps)[None, :] <= jnp.arange(steps)[:, None])[None, :, None, :]
        new_scores = jnp.where(causal, new_scores, negative)
        new_max = jnp.max(new_scores, axis=-1)
        new_weights = jnp.where(causal, jnp.exp(new_scores - new_max[..., None]), 0.0)
        new_total = jnp.sum(new_weights, axis=-1)
        new_out = jnp.einsum(
            "rsht,rtd->rshd",
            new_weights.astype(jnp.bfloat16),
            value_new.reshape(req_dev, steps, head_dim),
            preferred_element_type=jnp.float32,
        )
        overall = jnp.maximum(cache_max, new_max)
        src_scale = jnp.exp(got_max - overall[None])
        new_scale = jnp.exp(new_max - overall)
        total = jnp.sum(got_total * src_scale, axis=0) + new_total * new_scale
        summed = jnp.sum(got_out * src_scale[..., None], axis=0) + new_out * new_scale[..., None]
        attended = (
            (summed / total[..., None])
            .astype(jnp.bfloat16)
            .reshape(req_dev * steps, heads_dev * head_dim)
        )
        pair = [(i, i ^ 1) for i in range(tp_size)]
        quad = [(i, i ^ 2) for i in range(tp_size)]
        other_head = lax.ppermute(attended, "tp", pair)
        pair_heads = jnp.concatenate(
            [jnp.where(lower, attended, other_head), jnp.where(lower, other_head, attended)], axis=1
        )
        projected = jnp.dot(pair_heads, pair_weight, preferred_element_type=jnp.float32)
        far_heads = lax.ppermute(pair_heads, "tp", quad)
        projected = projected + jnp.dot(far_heads, far_weight, preferred_element_type=jnp.float32)
        attn_total = tree_sum(
            projected.astype(jnp.bfloat16), "tp", tp_size, first_step=4
        ).astype(jnp.float32)
        residual = (token_rows.astype(jnp.float32) + attn_total).astype(jnp.bfloat16)
        mlp_in = rms_norm(residual.astype(jnp.float32), mlp_gain).astype(jnp.bfloat16)
        gate = jnp.dot(mlp_in, gate_weight, preferred_element_type=jnp.float32)
        upward = jnp.dot(mlp_in, up_weight, preferred_element_type=jnp.float32)
        hidden = (jax.nn.gelu(gate, approximate=True) * upward).astype(jnp.bfloat16)
        mlp_part = jnp.dot(hidden, down_weight, preferred_element_type=jnp.float32).astype(
            jnp.bfloat16
        )
        mlp_total = tree_sum(mlp_part, "tp", tp_size).astype(jnp.float32)
        layer_out = (residual.astype(jnp.float32) + mlp_total).astype(jnp.bfloat16)
        return layer_out.reshape(req_dev, steps, width)

    return body


def solution(mesh):
    return jax.shard_map(
        make_body(mesh.shape["req"], mesh.shape["tp"]),
        mesh=mesh,
        in_specs=(
            P("req", None, None),
            P("req"),
            P("req", None),
            P("req", None, None, None),
            P(),
            P(None, "tp"),
            P(),
            P(),
            P("tp", None),
            P(),
            P(None, "tp"),
            P(None, "tp"),
            P("tp", None),
        ),
        out_specs=P("req", None, None),
        check_vma=False,
    )
```

```python
import jax
import jax.numpy as jnp
from jax import lax
from jax.sharding import PartitionSpec as P

WINDOW = 1024


negative = -1e30
epsilon = 1e-06


def rms_norm(values, gain):
    return values * lax.rsqrt(jnp.mean(values * values, axis=-1, keepdims=True) + epsilon) * gain


def tree_sum(values, axis, size, first_step=1):
    step = first_step
    while step < size // 2:
        values = values + lax.ppermute(values, axis, [(i, i ^ step) for i in range(size)])
        step *= 2
    if size > 1:
        values = values + lax.ppermute(values, axis, [(i, size - 1 - i) for i in range(size)])
    return values


def make_body(req_size, tp_size):
    def body(
        tokens,
        lengths,
        page_table,
        kv_pages,
        norm_gain,
        query_weight,
        key_weight,
        value_weight,
        out_weight,
        mlp_gain,
        gate_weight,
        up_weight,
        down_weight,
    ):
        req_dev, steps, width = tokens.shape
        head_dim = key_weight.shape[1]
        heads_dev = query_weight.shape[1] // head_dim
        pool_size = kv_pages.shape[0]
        page_size = kv_pages.shape[2]
        window_pages = page_table.shape[1]
        requests = req_dev * req_size
        qwidth = steps * heads_dev * head_dim
        token_rows = tokens.reshape(req_dev * steps, width)
        partner_weight = lax.ppermute(out_weight, "tp", [(i, i ^ 1) for i in range(tp_size)])
        far_weight = lax.ppermute(out_weight, "tp", [(i, i ^ 2) for i in range(tp_size)])
        far_partner_weight = lax.ppermute(out_weight, "tp", [(i, i ^ 3) for i in range(tp_size)])
        normed = rms_norm(token_rows.astype(jnp.float32), norm_gain).astype(jnp.bfloat16)
        queries = (
            jnp.dot(normed, query_weight, preferred_element_type=jnp.float32) * head_dim ** (-0.5)
        ).astype(jnp.bfloat16)
        key_new = jnp.dot(normed, key_weight, preferred_element_type=jnp.float32).astype(jnp.bfloat16)
        value_new = jnp.dot(normed, value_weight, preferred_element_type=jnp.float32).astype(
            jnp.bfloat16
        )
        length_col = jnp.broadcast_to(lengths[:, None], (req_dev, 1))
        packed = jnp.concatenate(
            [
                queries.reshape(req_dev, qwidth),
                (page_table // 256).astype(jnp.bfloat16),
                (length_col // 256).astype(jnp.bfloat16),
                (page_table % 256).astype(jnp.bfloat16),
                (length_col % 256).astype(jnp.bfloat16),
            ],
            axis=1,
        )
        gathered = lax.all_to_all(
            jnp.broadcast_to(packed[None], (req_size,) + packed.shape), "req", 0, 0, tiled=False
        ).reshape(requests, packed.shape[1])
        all_queries = gathered[:, :qwidth].reshape(requests, steps * heads_dev, head_dim)
        nints = window_pages + 1
        digits = gathered[:, qwidth:].astype(jnp.int32)
        all_ints = digits[:, :nints] * 256 + digits[:, nints:]
        all_table = all_ints[:, :window_pages]
        all_lengths = all_ints[:, window_pages]
        flat_table = all_table.reshape(-1)
        entries = flat_table.shape[0]
        my_slots = lax.axis_index("req") * pool_size + jnp.arange(pool_size, dtype=jnp.int32)
        match = flat_table[None, :] == my_slots[:, None]
        owner_entry = jnp.sum(
            jnp.where(match, jnp.arange(entries, dtype=jnp.int32)[None, :], 0), axis=1
        )
        page_request = owner_entry // window_pages
        page_number = owner_entry % window_pages
        entry_length = jnp.repeat(all_lengths, window_pages)
        page_length = jnp.sum(jnp.where(match, entry_length[None, :], 0), axis=1)
        first_page = jnp.maximum(page_length - (WINDOW - 1), 0) // page_size
        position = (first_page + page_number)[:, None] * page_size + jnp.arange(
            page_size, dtype=jnp.int32
        )[None, :]
        current = page_length[:, None] + jnp.arange(steps, dtype=jnp.int32)[None, :]
        visible = (position[:, None, :] < page_length[:, None, None]) & (
            position[:, None, :] > current[:, :, None] - WINDOW
        )
        visible = visible[:, :, None, :]
        page_queries = all_queries[page_request]
        scores = jnp.einsum(
            "pqd,pkd->pqk", page_queries, kv_pages[:, 0], preferred_element_type=jnp.float32
        )
        scores = jnp.where(visible, scores.reshape(pool_size, steps, heads_dev, page_size), negative)
        block_max = jnp.max(scores, axis=-1)
        weights = jnp.where(visible, jnp.exp(scores - block_max[..., None]), 0.0)
        block_total = jnp.sum(weights, axis=-1)
        block_out = jnp.einsum(
            "pqk,pkd->pqd",
            weights.astype(jnp.bfloat16).reshape(pool_size, steps * heads_dev, page_size),
            kv_pages[:, 1],
            preferred_element_type=jnp.float32,
        )
        block_out = block_out.reshape(pool_size, steps, heads_dev, head_dim)
        member = page_request[None, :] == jnp.arange(requests, dtype=jnp.int32)[:, None]
        local_max = jnp.max(
            jnp.where(member[:, :, None, None], block_max[None], negative), axis=1
        )
        same_request = page_request[:, None] == page_request[None, :]
        page_ref_max = jnp.max(
            jnp.where(same_request[:, :, None, None], block_max[None], negative), axis=1
        )
        scale = jnp.exp(block_max - page_ref_max)
        nsh = steps * heads_dev
        scaled = jnp.concatenate(
            [
                (block_out * scale[..., None]).reshape(pool_size, nsh * head_dim),
                (block_total * scale).reshape(pool_size, nsh),
            ],
            axis=1,
        )
        sent = jnp.dot(
            member.astype(jnp.float32),
            scaled,
            precision=lax.Precision.HIGHEST,
            preferred_element_type=jnp.float32,
        )
        flat_max = local_max.reshape(requests, nsh)
        max_hi = lax.reduce_precision(flat_max, exponent_bits=8, mantissa_bits=7)
        rest = flat_max - max_hi
        max_mid = lax.reduce_precision(rest, exponent_bits=8, mantissa_bits=7)
        max_lo = rest - max_mid
        send = jnp.concatenate(
            [sent, max_hi, max_mid, max_lo], axis=1
        ).astype(jnp.bfloat16)
        recv = lax.all_to_all(send, "req", 0, 0, tiled=True).reshape(req_size, req_dev, -1)
        got_out = (
            recv[:, :, : nsh * head_dim]
            .astype(jnp.float32)
            .reshape(req_size, req_dev, steps, heads_dev, head_dim)
        )
        got_total = (
            recv[:, :, nsh * head_dim : nsh * (head_dim + 1)]
            .astype(jnp.float32)
            .reshape(req_size, req_dev, steps, heads_dev)
        )
        pieces = recv[:, :, nsh * (head_dim + 1) :].astype(jnp.float32)
        got_max = (
            (pieces[:, :, :nsh] + pieces[:, :, nsh : 2 * nsh]) + pieces[:, :, 2 * nsh :]
        ).reshape(req_size, req_dev, steps, heads_dev)
        cache_max = jnp.max(got_max, axis=0)
        local_queries = queries.reshape(req_dev, steps, heads_dev, head_dim)
        new_scores = jnp.einsum(
            "rshd,rtd->rsht",
            local_queries,
            key_new.reshape(req_dev, steps, head_dim),
            preferred_element_type=jnp.float32,
        )
        causal = (jnp.arange(steps)[None, :] <= jnp.arange(steps)[:, None])[None, :, None, :]
        new_scores = jnp.where(causal, new_scores, negative)
        new_max = jnp.max(new_scores, axis=-1)
        new_weights = jnp.where(causal, jnp.exp(new_scores - new_max[..., None]), 0.0)
        new_total = jnp.sum(new_weights, axis=-1)
        new_out = jnp.einsum(
            "rsht,rtd->rshd",
            new_weights.astype(jnp.bfloat16),
            value_new.reshape(req_dev, steps, head_dim),
            preferred_element_type=jnp.float32,
        )
        overall = jnp.maximum(cache_max, new_max)
        src_scale = jnp.exp(got_max - overall[None])
        new_scale = jnp.exp(new_max - overall)
        total = jnp.sum(got_total * src_scale, axis=0) + new_total * new_scale
        summed = jnp.sum(got_out * src_scale[..., None], axis=0) + new_out * new_scale[..., None]
        attended = (
            (summed / total[..., None])
            .astype(jnp.bfloat16)
            .reshape(req_dev * steps, heads_dev * head_dim)
        )
        pair = [(i, i ^ 1) for i in range(tp_size)]
        other_head = lax.ppermute(attended, "tp", pair)
        projected = jnp.dot(attended, out_weight, preferred_element_type=jnp.float32) + jnp.dot(
            other_head, partner_weight, preferred_element_type=jnp.float32
        )
        far = lax.ppermute(
            jnp.concatenate([attended, other_head], axis=1), "tp", [(i, i ^ 2) for i in range(tp_size)]
        )
        far_width = attended.shape[1]
        projected = projected + (
            jnp.dot(far[:, :far_width], far_weight, preferred_element_type=jnp.float32)
            + jnp.dot(far[:, far_width:], far_partner_weight, preferred_element_type=jnp.float32)
        )
        attn_total = tree_sum(
            projected.astype(jnp.bfloat16), "tp", tp_size, first_step=4
        ).astype(jnp.float32)
        residual = (token_rows.astype(jnp.float32) + attn_total).astype(jnp.bfloat16)
        mlp_in = rms_norm(residual.astype(jnp.float32), mlp_gain).astype(jnp.bfloat16)
        gate = jnp.dot(mlp_in, gate_weight, preferred_element_type=jnp.float32)
        upward = jnp.dot(mlp_in, up_weight, preferred_element_type=jnp.float32)
        hidden = (jax.nn.gelu(gate, approximate=True) * upward).astype(jnp.bfloat16)
        mlp_part = jnp.dot(hidden, down_weight, preferred_element_type=jnp.float32).astype(
            jnp.bfloat16
        )
        mlp_total = tree_sum(mlp_part, "tp", tp_size).astype(jnp.float32)
        layer_out = (residual.astype(jnp.float32) + mlp_total).astype(jnp.bfloat16)
        return layer_out.reshape(req_dev, steps, width)

    return body


def solution(mesh):
    return jax.shard_map(
        make_body(mesh.shape["req"], mesh.shape["tp"]),
        mesh=mesh,
        in_specs=(
            P("req", None, None),
            P("req"),
            P("req", None),
            P("req", None, None, None),
            P(),
            P(None, "tp"),
            P(),
            P(),
            P("tp", None),
            P(),
            P(None, "tp"),
            P(None, "tp"),
            P("tp", None),
        ),
        out_specs=P("req", None, None),
        check_vma=False,
    )
```

```python
import jax
import jax.numpy as jnp
from jax import lax
from jax.sharding import PartitionSpec as P

WINDOW = 1024


negative = -1e30
epsilon = 1e-06


def rms_norm(values, gain):
    return values * lax.rsqrt(jnp.mean(values * values, axis=-1, keepdims=True) + epsilon) * gain


def tree_sum(values, axis, size, first_step=1):
    step = first_step
    while step < size // 2:
        values = values + lax.ppermute(values, axis, [(i, i ^ step) for i in range(size)])
        step *= 2
    if size > 1:
        values = values + lax.ppermute(values, axis, [(i, size - 1 - i) for i in range(size)])
    return values


def make_body(req_size, tp_size):
    def body(
        tokens,
        lengths,
        page_table,
        kv_pages,
        norm_gain,
        query_weight,
        key_weight,
        value_weight,
        out_weight,
        mlp_gain,
        gate_weight,
        up_weight,
        down_weight,
    ):
        req_dev, steps, width = tokens.shape
        head_dim = key_weight.shape[1]
        heads_dev = query_weight.shape[1] // head_dim
        pool_size = kv_pages.shape[0]
        page_size = kv_pages.shape[2]
        window_pages = page_table.shape[1]
        requests = req_dev * req_size
        qwidth = steps * heads_dev * head_dim
        token_rows = tokens.reshape(req_dev * steps, width)
        partner_weight = lax.ppermute(out_weight, "tp", [(i, i ^ 1) for i in range(tp_size)])
        partner_down = lax.ppermute(down_weight, "tp", [(i, i ^ 1) for i in range(tp_size)])
        normed = rms_norm(token_rows.astype(jnp.float32), norm_gain).astype(jnp.bfloat16)
        queries = (
            jnp.dot(normed, query_weight, preferred_element_type=jnp.float32) * head_dim ** (-0.5)
        ).astype(jnp.bfloat16)
        key_new = jnp.dot(normed, key_weight, preferred_element_type=jnp.float32).astype(jnp.bfloat16)
        value_new = jnp.dot(normed, value_weight, preferred_element_type=jnp.float32).astype(
            jnp.bfloat16
        )
        length_col = jnp.broadcast_to(lengths[:, None], (req_dev, 1))
        packed = jnp.concatenate(
            [
                queries.reshape(req_dev, qwidth),
                (page_table // 256).astype(jnp.bfloat16),
                (length_col // 256).astype(jnp.bfloat16),
                (page_table % 256).astype(jnp.bfloat16),
                (length_col % 256).astype(jnp.bfloat16),
            ],
            axis=1,
        )
        gathered = lax.all_to_all(
            jnp.broadcast_to(packed[None], (req_size,) + packed.shape), "req", 0, 0, tiled=False
        ).reshape(requests, packed.shape[1])
        all_queries = gathered[:, :qwidth].reshape(requests, steps * heads_dev, head_dim)
        nints = window_pages + 1
        digits = gathered[:, qwidth:].astype(jnp.int32)
        all_ints = digits[:, :nints] * 256 + digits[:, nints:]
        all_table = all_ints[:, :window_pages]
        all_lengths = all_ints[:, window_pages]
        flat_table = all_table.reshape(-1)
        entries = flat_table.shape[0]
        my_slots = lax.axis_index("req") * pool_size + jnp.arange(pool_size, dtype=jnp.int32)
        match = flat_table[None, :] == my_slots[:, None]
        owner_entry = jnp.sum(
            jnp.where(match, jnp.arange(entries, dtype=jnp.int32)[None, :], 0), axis=1
        )
        page_request = owner_entry // window_pages
        page_number = owner_entry % window_pages
        entry_length = jnp.repeat(all_lengths, window_pages)
        page_length = jnp.sum(jnp.where(match, entry_length[None, :], 0), axis=1)
        first_page = jnp.maximum(page_length - (WINDOW - 1), 0) // page_size
        position = (first_page + page_number)[:, None] * page_size + jnp.arange(
            page_size, dtype=jnp.int32
        )[None, :]
        current = page_length[:, None] + jnp.arange(steps, dtype=jnp.int32)[None, :]
        visible = (position[:, None, :] < page_length[:, None, None]) & (
            position[:, None, :] > current[:, :, None] - WINDOW
        )
        visible = visible[:, :, None, :]
        page_queries = all_queries[page_request]
        scores = jnp.einsum(
            "pqd,pkd->pqk", page_queries, kv_pages[:, 0], preferred_element_type=jnp.float32
        )
        scores = jnp.where(visible, scores.reshape(pool_size, steps, heads_dev, page_size), negative)
        block_max = jnp.max(scores, axis=-1)
        weights = jnp.where(visible, jnp.exp(scores - block_max[..., None]), 0.0)
        block_total = jnp.sum(weights, axis=-1)
        block_out = jnp.einsum(
            "pqk,pkd->pqd",
            weights.astype(jnp.bfloat16).reshape(pool_size, steps * heads_dev, page_size),
            kv_pages[:, 1],
            preferred_element_type=jnp.float32,
        )
        block_out = block_out.reshape(pool_size, steps, heads_dev, head_dim)
        member = page_request[None, :] == jnp.arange(requests, dtype=jnp.int32)[:, None]
        local_max = jnp.max(
            jnp.where(member[:, :, None, None], block_max[None], negative), axis=1
        )
        same_request = page_request[:, None] == page_request[None, :]
        page_ref_max = jnp.max(
            jnp.where(same_request[:, :, None, None], block_max[None], negative), axis=1
        )
        scale = jnp.exp(block_max - page_ref_max)
        nsh = steps * heads_dev
        scaled = jnp.concatenate(
            [
                (block_out * scale[..., None]).reshape(pool_size, nsh * head_dim),
                (block_total * scale).reshape(pool_size, nsh),
            ],
            axis=1,
        )
        sent = jnp.dot(
            member.astype(jnp.float32),
            scaled,
            precision=lax.Precision.HIGHEST,
            preferred_element_type=jnp.float32,
        )
        flat_max = local_max.reshape(requests, nsh)
        max_hi = lax.reduce_precision(flat_max, exponent_bits=8, mantissa_bits=7)
        rest = flat_max - max_hi
        max_mid = lax.reduce_precision(rest, exponent_bits=8, mantissa_bits=7)
        max_lo = rest - max_mid
        send = jnp.concatenate(
            [sent, max_hi, max_mid, max_lo], axis=1
        ).astype(jnp.bfloat16)
        recv = lax.all_to_all(send, "req", 0, 0, tiled=True).reshape(req_size, req_dev, -1)
        got_out = (
            recv[:, :, : nsh * head_dim]
            .astype(jnp.float32)
            .reshape(req_size, req_dev, steps, heads_dev, head_dim)
        )
        got_total = (
            recv[:, :, nsh * head_dim : nsh * (head_dim + 1)]
            .astype(jnp.float32)
            .reshape(req_size, req_dev, steps, heads_dev)
        )
        pieces = recv[:, :, nsh * (head_dim + 1) :].astype(jnp.float32)
        got_max = (
            (pieces[:, :, :nsh] + pieces[:, :, nsh : 2 * nsh]) + pieces[:, :, 2 * nsh :]
        ).reshape(req_size, req_dev, steps, heads_dev)
        cache_max = jnp.max(got_max, axis=0)
        local_queries = queries.reshape(req_dev, steps, heads_dev, head_dim)
        new_scores = jnp.einsum(
            "rshd,rtd->rsht",
            local_queries,
            key_new.reshape(req_dev, steps, head_dim),
            preferred_element_type=jnp.float32,
        )
        causal = (jnp.arange(steps)[None, :] <= jnp.arange(steps)[:, None])[None, :, None, :]
        new_scores = jnp.where(causal, new_scores, negative)
        new_max = jnp.max(new_scores, axis=-1)
        new_weights = jnp.where(causal, jnp.exp(new_scores - new_max[..., None]), 0.0)
        new_total = jnp.sum(new_weights, axis=-1)
        new_out = jnp.einsum(
            "rsht,rtd->rshd",
            new_weights.astype(jnp.bfloat16),
            value_new.reshape(req_dev, steps, head_dim),
            preferred_element_type=jnp.float32,
        )
        overall = jnp.maximum(cache_max, new_max)
        src_scale = jnp.exp(got_max - overall[None])
        new_scale = jnp.exp(new_max - overall)
        total = jnp.sum(got_total * src_scale, axis=0) + new_total * new_scale
        summed = jnp.sum(got_out * src_scale[..., None], axis=0) + new_out * new_scale[..., None]
        attended = (
            (summed / total[..., None])
            .astype(jnp.bfloat16)
            .reshape(req_dev * steps, heads_dev * head_dim)
        )
        pair = [(i, i ^ 1) for i in range(tp_size)]
        other_head = lax.ppermute(attended, "tp", pair)
        lower = lax.axis_index("tp") % 2 == 0
        pair_heads = jnp.concatenate(
            [jnp.where(lower, attended, other_head), jnp.where(lower, other_head, attended)], axis=1
        )
        pair_weight = jnp.concatenate(
            [jnp.where(lower, out_weight, partner_weight), jnp.where(lower, partner_weight, out_weight)],
            axis=0,
        )
        projected = jnp.dot(pair_heads, pair_weight, preferred_element_type=jnp.float32)
        attn_total = tree_sum(
            projected.astype(jnp.bfloat16), "tp", tp_size, first_step=2
        ).astype(jnp.float32)
        residual = (token_rows.astype(jnp.float32) + attn_total).astype(jnp.bfloat16)
        mlp_in = rms_norm(residual.astype(jnp.float32), mlp_gain).astype(jnp.bfloat16)
        gate = jnp.dot(mlp_in, gate_weight, preferred_element_type=jnp.float32)
        upward = jnp.dot(mlp_in, up_weight, preferred_element_type=jnp.float32)
        hidden = (jax.nn.gelu(gate, approximate=True) * upward).astype(jnp.bfloat16)
        other_hidden = lax.ppermute(hidden, "tp", [(i, i ^ 1) for i in range(tp_size)])
        mlp_part = (
            jnp.dot(hidden, down_weight, preferred_element_type=jnp.float32)
            + jnp.dot(other_hidden, partner_down, preferred_element_type=jnp.float32)
        ).astype(jnp.bfloat16)
        mlp_total = tree_sum(mlp_part, "tp", tp_size, first_step=2).astype(jnp.float32)
        layer_out = (residual.astype(jnp.float32) + mlp_total).astype(jnp.bfloat16)
        return layer_out.reshape(req_dev, steps, width)

    return body


def solution(mesh):
    return jax.shard_map(
        make_body(mesh.shape["req"], mesh.shape["tp"]),
        mesh=mesh,
        in_specs=(
            P("req", None, None),
            P("req"),
            P("req", None),
            P("req", None, None, None),
            P(),
            P(None, "tp"),
            P(),
            P(),
            P("tp", None),
            P(),
            P(None, "tp"),
            P(None, "tp"),
            P("tp", None),
        ),
        out_specs=P("req", None, None),
        check_vma=False,
    )
```

```python
import jax
import jax.numpy as jnp
from jax import lax
from jax.sharding import PartitionSpec as P

WINDOW = 1024


negative = -1e30
epsilon = 1e-06


def rms_norm(values, gain):
    return values * lax.rsqrt(jnp.mean(values * values, axis=-1, keepdims=True) + epsilon) * gain


def tree_sum(values, axis, size, first_step=1):
    step = first_step
    while step < size // 2:
        values = values + lax.ppermute(values, axis, [(i, i ^ (2 * step - 1)) for i in range(size)])
        step *= 2
    if size > 1:
        values = values + lax.ppermute(values, axis, [(i, size - 1 - i) for i in range(size)])
    return values


def make_body(req_size, tp_size):
    def body(
        tokens,
        lengths,
        page_table,
        kv_pages,
        norm_gain,
        query_weight,
        key_weight,
        value_weight,
        out_weight,
        mlp_gain,
        gate_weight,
        up_weight,
        down_weight,
    ):
        req_dev, steps, width = tokens.shape
        head_dim = key_weight.shape[1]
        heads_dev = query_weight.shape[1] // head_dim
        pool_size = kv_pages.shape[0]
        page_size = kv_pages.shape[2]
        window_pages = page_table.shape[1]
        requests = req_dev * req_size
        qwidth = steps * heads_dev * head_dim
        token_rows = tokens.reshape(req_dev * steps, width)
        partner_weight = lax.ppermute(out_weight, "tp", [(i, i ^ 1) for i in range(tp_size)])
        normed = rms_norm(token_rows.astype(jnp.float32), norm_gain).astype(jnp.bfloat16)
        queries = (
            jnp.dot(normed, query_weight, preferred_element_type=jnp.float32) * head_dim ** (-0.5)
        ).astype(jnp.bfloat16)
        key_new = jnp.dot(normed, key_weight, preferred_element_type=jnp.float32).astype(jnp.bfloat16)
        value_new = jnp.dot(normed, value_weight, preferred_element_type=jnp.float32).astype(
            jnp.bfloat16
        )
        length_col = jnp.broadcast_to(lengths[:, None], (req_dev, 1))
        packed = jnp.concatenate(
            [
                queries.reshape(req_dev, qwidth),
                (page_table // 256).astype(jnp.bfloat16),
                (length_col // 256).astype(jnp.bfloat16),
                (page_table % 256).astype(jnp.bfloat16),
                (length_col % 256).astype(jnp.bfloat16),
            ],
            axis=1,
        )
        gathered = lax.all_to_all(
            jnp.broadcast_to(packed[None], (req_size,) + packed.shape), "req", 0, 0, tiled=False
        ).reshape(requests, packed.shape[1])
        all_queries = gathered[:, :qwidth].reshape(requests, steps * heads_dev, head_dim)
        nints = window_pages + 1
        digits = gathered[:, qwidth:].astype(jnp.int32)
        all_ints = digits[:, :nints] * 256 + digits[:, nints:]
        all_table = all_ints[:, :window_pages]
        all_lengths = all_ints[:, window_pages]
        flat_table = all_table.reshape(-1)
        entries = flat_table.shape[0]
        my_slots = lax.axis_index("req") * pool_size + jnp.arange(pool_size, dtype=jnp.int32)
        match = flat_table[None, :] == my_slots[:, None]
        owner_entry = jnp.sum(
            jnp.where(match, jnp.arange(entries, dtype=jnp.int32)[None, :], 0), axis=1
        )
        page_request = owner_entry // window_pages
        page_number = owner_entry % window_pages
        entry_length = jnp.repeat(all_lengths, window_pages)
        page_length = jnp.sum(jnp.where(match, entry_length[None, :], 0), axis=1)
        first_page = jnp.maximum(page_length - (WINDOW - 1), 0) // page_size
        position = (first_page + page_number)[:, None] * page_size + jnp.arange(
            page_size, dtype=jnp.int32
        )[None, :]
        current = page_length[:, None] + jnp.arange(steps, dtype=jnp.int32)[None, :]
        visible = (position[:, None, :] < page_length[:, None, None]) & (
            position[:, None, :] > current[:, :, None] - WINDOW
        )
        visible = visible[:, :, None, :]
        page_queries = all_queries[page_request]
        scores = jnp.einsum(
            "pqd,pkd->pqk", page_queries, kv_pages[:, 0], preferred_element_type=jnp.float32
        )
        scores = jnp.where(visible, scores.reshape(pool_size, steps, heads_dev, page_size), negative)
        block_max = jnp.max(scores, axis=-1)
        weights = jnp.where(visible, jnp.exp(scores - block_max[..., None]), 0.0)
        block_total = jnp.sum(weights, axis=-1)
        block_out = jnp.einsum(
            "pqk,pkd->pqd",
            weights.astype(jnp.bfloat16).reshape(pool_size, steps * heads_dev, page_size),
            kv_pages[:, 1],
            preferred_element_type=jnp.float32,
        )
        block_out = block_out.reshape(pool_size, steps, heads_dev, head_dim)
        member = page_request[None, :] == jnp.arange(requests, dtype=jnp.int32)[:, None]
        local_max = jnp.max(
            jnp.where(member[:, :, None, None], block_max[None], negative), axis=1
        )
        same_request = page_request[:, None] == page_request[None, :]
        page_ref_max = jnp.max(
            jnp.where(same_request[:, :, None, None], block_max[None], negative), axis=1
        )
        scale = jnp.exp(block_max - page_ref_max)
        nsh = steps * heads_dev
        scaled = jnp.concatenate(
            [
                (block_out * scale[..., None]).reshape(pool_size, nsh * head_dim),
                (block_total * scale).reshape(pool_size, nsh),
            ],
            axis=1,
        )
        sent = jnp.dot(
            member.astype(jnp.float32),
            scaled,
            precision=lax.Precision.HIGHEST,
            preferred_element_type=jnp.float32,
        )
        flat_max = local_max.reshape(requests, nsh)
        max_hi = lax.reduce_precision(flat_max, exponent_bits=8, mantissa_bits=7)
        rest = flat_max - max_hi
        max_mid = lax.reduce_precision(rest, exponent_bits=8, mantissa_bits=7)
        max_lo = rest - max_mid
        send = jnp.concatenate(
            [sent, max_hi, max_mid, max_lo], axis=1
        ).astype(jnp.bfloat16)
        recv = lax.all_to_all(send, "req", 0, 0, tiled=True).reshape(req_size, req_dev, -1)
        got_out = (
            recv[:, :, : nsh * head_dim]
            .astype(jnp.float32)
            .reshape(req_size, req_dev, steps, heads_dev, head_dim)
        )
        got_total = (
            recv[:, :, nsh * head_dim : nsh * (head_dim + 1)]
            .astype(jnp.float32)
            .reshape(req_size, req_dev, steps, heads_dev)
        )
        pieces = recv[:, :, nsh * (head_dim + 1) :].astype(jnp.float32)
        got_max = (
            (pieces[:, :, :nsh] + pieces[:, :, nsh : 2 * nsh]) + pieces[:, :, 2 * nsh :]
        ).reshape(req_size, req_dev, steps, heads_dev)
        cache_max = jnp.max(got_max, axis=0)
        local_queries = queries.reshape(req_dev, steps, heads_dev, head_dim)
        new_scores = jnp.einsum(
            "rshd,rtd->rsht",
            local_queries,
            key_new.reshape(req_dev, steps, head_dim),
            preferred_element_type=jnp.float32,
        )
        causal = (jnp.arange(steps)[None, :] <= jnp.arange(steps)[:, None])[None, :, None, :]
        new_scores = jnp.where(causal, new_scores, negative)
        new_max = jnp.max(new_scores, axis=-1)
        new_weights = jnp.where(causal, jnp.exp(new_scores - new_max[..., None]), 0.0)
        new_total = jnp.sum(new_weights, axis=-1)
        new_out = jnp.einsum(
            "rsht,rtd->rshd",
            new_weights.astype(jnp.bfloat16),
            value_new.reshape(req_dev, steps, head_dim),
            preferred_element_type=jnp.float32,
        )
        overall = jnp.maximum(cache_max, new_max)
        src_scale = jnp.exp(got_max - overall[None])
        new_scale = jnp.exp(new_max - overall)
        total = jnp.sum(got_total * src_scale, axis=0) + new_total * new_scale
        summed = jnp.sum(got_out * src_scale[..., None], axis=0) + new_out * new_scale[..., None]
        attended = (
            (summed / total[..., None])
            .astype(jnp.bfloat16)
            .reshape(req_dev * steps, heads_dev * head_dim)
        )
        pair = [(i, i ^ 1) for i in range(tp_size)]
        other_head = lax.ppermute(attended, "tp", pair)
        lower = lax.axis_index("tp") % 2 == 0
        pair_heads = jnp.concatenate(
            [jnp.where(lower, attended, other_head), jnp.where(lower, other_head, attended)], axis=1
        )
        pair_weight = jnp.concatenate(
            [jnp.where(lower, out_weight, partner_weight), jnp.where(lower, partner_weight, out_weight)],
            axis=0,
        )
        projected = jnp.dot(pair_heads, pair_weight, preferred_element_type=jnp.float32)
        attn_total = tree_sum(
            projected.astype(jnp.bfloat16), "tp", tp_size, first_step=2
        ).astype(jnp.float32)
        residual = (token_rows.astype(jnp.float32) + attn_total).astype(jnp.bfloat16)
        mlp_in = rms_norm(residual.astype(jnp.float32), mlp_gain).astype(jnp.bfloat16)
        gate = jnp.dot(mlp_in, gate_weight, preferred_element_type=jnp.float32)
        upward = jnp.dot(mlp_in, up_weight, preferred_element_type=jnp.float32)
        hidden = (jax.nn.gelu(gate, approximate=True) * upward).astype(jnp.bfloat16)
        mlp_part = jnp.dot(hidden, down_weight, preferred_element_type=jnp.float32).astype(
            jnp.bfloat16
        )
        mlp_total = tree_sum(mlp_part, "tp", tp_size).astype(jnp.float32)
        layer_out = (residual.astype(jnp.float32) + mlp_total).astype(jnp.bfloat16)
        return layer_out.reshape(req_dev, steps, width)

    return body


def solution(mesh):
    return jax.shard_map(
        make_body(mesh.shape["req"], mesh.shape["tp"]),
        mesh=mesh,
        in_specs=(
            P("req", None, None),
            P("req"),
            P("req", None),
            P("req", None, None, None),
            P(),
            P(None, "tp"),
            P(),
            P(),
            P("tp", None),
            P(),
            P(None, "tp"),
            P(None, "tp"),
            P("tp", None),
        ),
        out_specs=P("req", None, None),
        check_vma=False,
    )
```

```python
import jax
import jax.numpy as jnp
from jax import lax
from jax.sharding import PartitionSpec as P

WINDOW = 1024


negative = -1e30
epsilon = 1e-06


def rms_norm(values, gain):
    return values * lax.rsqrt(jnp.mean(values * values, axis=-1, keepdims=True) + epsilon) * gain


def tree_sum(values, axis, size, first_step=1):
    step = first_step
    while step < size // 2:
        values = values + lax.ppermute(values, axis, [(i, i ^ (2 * step - 1)) for i in range(size)])
        step *= 2
    if size > 1:
        values = values + lax.ppermute(values, axis, [(i, size - 1 - i) for i in range(size)])
    return values


def make_body(req_size, tp_size):
    def body(
        tokens,
        lengths,
        page_table,
        kv_pages,
        norm_gain,
        query_weight,
        key_weight,
        value_weight,
        out_weight,
        mlp_gain,
        gate_weight,
        up_weight,
        down_weight,
    ):
        req_dev, steps, width = tokens.shape
        head_dim = key_weight.shape[1]
        heads_dev = query_weight.shape[1] // head_dim
        pool_size = kv_pages.shape[0]
        page_size = kv_pages.shape[2]
        window_pages = page_table.shape[1]
        requests = req_dev * req_size
        qwidth = steps * heads_dev * head_dim
        token_rows = tokens.reshape(req_dev * steps, width)
        partner_weight = lax.ppermute(out_weight, "tp", [(i, i ^ 1) for i in range(tp_size)])
        normed = rms_norm(token_rows.astype(jnp.float32), norm_gain).astype(jnp.bfloat16)
        queries = (
            jnp.dot(normed, query_weight, preferred_element_type=jnp.float32) * head_dim ** (-0.5)
        ).astype(jnp.bfloat16)
        key_new = jnp.dot(normed, key_weight, preferred_element_type=jnp.float32).astype(jnp.bfloat16)
        value_new = jnp.dot(normed, value_weight, preferred_element_type=jnp.float32).astype(
            jnp.bfloat16
        )
        length_col = jnp.broadcast_to(lengths[:, None], (req_dev, 1))
        packed = jnp.concatenate(
            [
                queries.reshape(req_dev, qwidth),
                (page_table // 256).astype(jnp.bfloat16),
                (length_col // 256).astype(jnp.bfloat16),
                (page_table % 256).astype(jnp.bfloat16),
                (length_col % 256).astype(jnp.bfloat16),
            ],
            axis=1,
        )
        gathered = lax.all_to_all(
            jnp.broadcast_to(packed[None], (req_size,) + packed.shape), "req", 0, 0, tiled=False
        ).reshape(requests, packed.shape[1])
        all_queries = gathered[:, :qwidth].reshape(requests, steps * heads_dev, head_dim)
        nints = window_pages + 1
        digits = gathered[:, qwidth:].astype(jnp.int32)
        all_ints = digits[:, :nints] * 256 + digits[:, nints:]
        all_table = all_ints[:, :window_pages]
        all_lengths = all_ints[:, window_pages]
        flat_table = all_table.reshape(-1)
        entries = flat_table.shape[0]
        my_slots = lax.axis_index("req") * pool_size + jnp.arange(pool_size, dtype=jnp.int32)
        match = flat_table[None, :] == my_slots[:, None]
        owner_entry = jnp.sum(
            jnp.where(match, jnp.arange(entries, dtype=jnp.int32)[None, :], 0), axis=1
        )
        page_request = owner_entry // window_pages
        page_number = owner_entry % window_pages
        entry_length = jnp.repeat(all_lengths, window_pages)
        page_length = jnp.sum(jnp.where(match, entry_length[None, :], 0), axis=1)
        first_page = jnp.maximum(page_length - (WINDOW - 1), 0) // page_size
        position = (first_page + page_number)[:, None] * page_size + jnp.arange(
            page_size, dtype=jnp.int32
        )[None, :]
        current = page_length[:, None] + jnp.arange(steps, dtype=jnp.int32)[None, :]
        visible = (position[:, None, :] < page_length[:, None, None]) & (
            position[:, None, :] > current[:, :, None] - WINDOW
        )
        visible = visible[:, :, None, :]
        page_queries = all_queries[page_request]
        scores = jnp.einsum(
            "pqd,pkd->pqk", page_queries, kv_pages[:, 0], preferred_element_type=jnp.float32
        )
        scores = jnp.where(visible, scores.reshape(pool_size, steps, heads_dev, page_size), negative)
        block_max = jnp.max(scores, axis=-1)
        weights = jnp.where(visible, jnp.exp(scores - block_max[..., None]), 0.0)
        block_total = jnp.sum(weights, axis=-1)
        block_out = jnp.einsum(
            "pqk,pkd->pqd",
            weights.astype(jnp.bfloat16).reshape(pool_size, steps * heads_dev, page_size),
            kv_pages[:, 1],
            preferred_element_type=jnp.float32,
        )
        block_out = block_out.reshape(pool_size, steps, heads_dev, head_dim)
        member = page_request[None, :] == jnp.arange(requests, dtype=jnp.int32)[:, None]
        local_max = jnp.max(
            jnp.where(member[:, :, None, None], block_max[None], negative), axis=1
        )
        same_request = page_request[:, None] == page_request[None, :]
        page_ref_max = jnp.max(
            jnp.where(same_request[:, :, None, None], block_max[None], negative), axis=1
        )
        scale = jnp.exp(block_max - page_ref_max)
        nsh = steps * heads_dev
        scaled = jnp.concatenate(
            [
                (block_out * scale[..., None]).reshape(pool_size, nsh * head_dim),
                (block_total * scale).reshape(pool_size, nsh),
            ],
            axis=1,
        )
        sent = jnp.dot(
            member.astype(jnp.float32),
            scaled,
            precision=lax.Precision.HIGH,
            preferred_element_type=jnp.float32,
        )
        flat_max = local_max.reshape(requests, nsh)
        max_hi = lax.reduce_precision(flat_max, exponent_bits=8, mantissa_bits=7)
        rest = flat_max - max_hi
        max_mid = lax.reduce_precision(rest, exponent_bits=8, mantissa_bits=7)
        max_lo = rest - max_mid
        send = jnp.concatenate(
            [sent, max_hi, max_mid, max_lo], axis=1
        ).astype(jnp.bfloat16)
        recv = lax.all_to_all(send, "req", 0, 0, tiled=True).reshape(req_size, req_dev, -1)
        got_out = (
            recv[:, :, : nsh * head_dim]
            .astype(jnp.float32)
            .reshape(req_size, req_dev, steps, heads_dev, head_dim)
        )
        got_total = (
            recv[:, :, nsh * head_dim : nsh * (head_dim + 1)]
            .astype(jnp.float32)
            .reshape(req_size, req_dev, steps, heads_dev)
        )
        pieces = recv[:, :, nsh * (head_dim + 1) :].astype(jnp.float32)
        got_max = (
            (pieces[:, :, :nsh] + pieces[:, :, nsh : 2 * nsh]) + pieces[:, :, 2 * nsh :]
        ).reshape(req_size, req_dev, steps, heads_dev)
        cache_max = jnp.max(got_max, axis=0)
        local_queries = queries.reshape(req_dev, steps, heads_dev, head_dim)
        new_scores = jnp.einsum(
            "rshd,rtd->rsht",
            local_queries,
            key_new.reshape(req_dev, steps, head_dim),
            preferred_element_type=jnp.float32,
        )
        causal = (jnp.arange(steps)[None, :] <= jnp.arange(steps)[:, None])[None, :, None, :]
        new_scores = jnp.where(causal, new_scores, negative)
        new_max = jnp.max(new_scores, axis=-1)
        new_weights = jnp.where(causal, jnp.exp(new_scores - new_max[..., None]), 0.0)
        new_total = jnp.sum(new_weights, axis=-1)
        new_out = jnp.einsum(
            "rsht,rtd->rshd",
            new_weights.astype(jnp.bfloat16),
            value_new.reshape(req_dev, steps, head_dim),
            preferred_element_type=jnp.float32,
        )
        overall = jnp.maximum(cache_max, new_max)
        src_scale = jnp.exp(got_max - overall[None])
        new_scale = jnp.exp(new_max - overall)
        total = jnp.sum(got_total * src_scale, axis=0) + new_total * new_scale
        summed = jnp.sum(got_out * src_scale[..., None], axis=0) + new_out * new_scale[..., None]
        attended = (
            (summed / total[..., None])
            .astype(jnp.bfloat16)
            .reshape(req_dev * steps, heads_dev * head_dim)
        )
        pair = [(i, i ^ 1) for i in range(tp_size)]
        other_head = lax.ppermute(attended, "tp", pair)
        lower = lax.axis_index("tp") % 2 == 0
        pair_heads = jnp.concatenate(
            [jnp.where(lower, attended, other_head), jnp.where(lower, other_head, attended)], axis=1
        )
        pair_weight = jnp.concatenate(
            [jnp.where(lower, out_weight, partner_weight), jnp.where(lower, partner_weight, out_weight)],
            axis=0,
        )
        projected = jnp.dot(pair_heads, pair_weight, preferred_element_type=jnp.float32)
        attn_total = tree_sum(
            projected.astype(jnp.bfloat16), "tp", tp_size, first_step=2
        ).astype(jnp.float32)
        residual = (token_rows.astype(jnp.float32) + attn_total).astype(jnp.bfloat16)
        mlp_in = rms_norm(residual.astype(jnp.float32), mlp_gain).astype(jnp.bfloat16)
        gate = jnp.dot(mlp_in, gate_weight, preferred_element_type=jnp.float32)
        upward = jnp.dot(mlp_in, up_weight, preferred_element_type=jnp.float32)
        hidden = (jax.nn.gelu(gate, approximate=True) * upward).astype(jnp.bfloat16)
        mlp_part = jnp.dot(hidden, down_weight, preferred_element_type=jnp.float32).astype(
            jnp.bfloat16
        )
        mlp_total = tree_sum(mlp_part, "tp", tp_size).astype(jnp.float32)
        layer_out = (residual.astype(jnp.float32) + mlp_total).astype(jnp.bfloat16)
        return layer_out.reshape(req_dev, steps, width)

    return body


def solution(mesh):
    return jax.shard_map(
        make_body(mesh.shape["req"], mesh.shape["tp"]),
        mesh=mesh,
        in_specs=(
            P("req", None, None),
            P("req"),
            P("req", None),
            P("req", None, None, None),
            P(),
            P(None, "tp"),
            P(),
            P(),
            P("tp", None),
            P(),
            P(None, "tp"),
            P(None, "tp"),
            P("tp", None),
        ),
        out_specs=P("req", None, None),
        check_vma=False,
    )
```
